256 devices in a mesh: blk: 128 (over z, x_hi, y, core), rows: 2 (over x_lo).
Axes of the slice: x: 4 (x_hi: 2, x_lo: 2; x = x_hi * 2 + x_lo), y: 4, z: 8, core: 2. Of those that a mesh axis runs over, the one named last changes fastest.
Arguments:
- tokens: bfloat16 [512, 8192], P(('blk', 'rows')), may hold values from -60 to 60
- norm_gain: float32 [8192], replicated, may hold values from 0.1 to 1.9
- gate_weight: bfloat16 [8192, 32768], P(None, 'blk'), may hold values from -0.09375 to 0.09375
- up_weight: bfloat16 [8192, 32768], P(None, 'blk'), may hold values from -0.09375 to 0.09375
- down_weight: bfloat16 [32768, 8192], P('blk'), may hold values from -0.046875 to 0.046875
- gate_mask: int32 [64, 256], P(None, 'blk'), may hold values from 0 to 1, as said below
- up_mask: int32 [64, 256], P(None, 'blk'), may hold values from 0 to 1, as said below
- down_mask: int32 [256, 64], P('blk'), may hold values 0 or 1
Outputs:
- ffn_out: bfloat16 [512, 8192], P(('blk', 'rows'))
The draws below stay inside these ranges and needn't reach their ends.
Inputs may be any that keep to these rules, and one draw needn't show every extreme that they name: Each column of gate_mask (64 block flags) has between 16 and 48 ones, and some column has exactly 48. Each column of up_mask (64 block flags) has between 16 and 48 ones, and some column has exactly 48.
All inputs are finite; a program needn't handle non-finite values. No bound on the sum of `down_mask` on one device may be relied on, other than what follows from the above.
Results may differ from the reference program's by a relative error of at most 0.0065.
Values may be sent and summed in bfloat16 or wider, within the bound.
No kernel may reach another device: no remote copies, remote signals or barrier semaphores. Data moves between devices by JAX's collectives and lax.ppermute only.
A program may use at most 128 MiB of HBM per device.

```python
import math
import jax
import jax.numpy as jnp
from jax import lax

D = 8192
PANEL = 256
FF = 32768
BLOCK = 128
RB = 64
FB = 256
KEEP_LEAST = 16
KEEP_MOST = 48
TOKENS = 512


def draw_tokens(key, part):
    key_base, key_rows, key_cols = jax.random.split(key, 3)
    row_scale = jnp.exp(jax.random.uniform(key_rows, (TOKENS, 1), jnp.float32, math.log(0.3), math.log(3.0)))
    col_scale = jnp.exp(jax.random.uniform(key_cols, (1, D), jnp.float32, math.log(0.3), math.log(3.0)))
    base = jnp.clip(jax.random.normal(key_base, (TOKENS, D), jnp.float32), -6.0, 6.0)
    return (base * row_scale * col_scale).astype(jnp.bfloat16)


def block_flags(key):
    key_count, key_which, key_score = jax.random.split(key, 3)
    counts = jax.random.randint(key_count, (FB,), KEEP_LEAST, KEEP_MOST + 1)
    which = jax.random.randint(key_which, (), 0, FB)
    counts = jnp.where(jnp.arange(FB) == which, KEEP_MOST, counts)
    scores = jax.random.randint(key_score, (RB, FB), 0, 1 << 20) * RB + jnp.arange(RB)[:, None]
    ranks = jnp.argsort(jnp.argsort(scores, axis=0), axis=0)
    return (ranks < counts[None, :]).astype(jnp.int32)


def draw_gate_mask(key, part):
    return block_flags(jax.random.fold_in(key, 11))


def draw_up_mask(key, part):
    return block_flags(jax.random.fold_in(key, 23))


def with_ends(result, key, smallest, largest):
    longest = result.shape.index(max(result.shape))
    spots = []
    for shift in (0, 1):
        where = [jax.random.randint(jax.random.fold_in(key, axis), (), 0, length) for axis, length in enumerate(result.shape)]
        where[longest] = (where[longest] + shift) % result.shape[longest]
        spots.append(tuple(where))
    return result.at[spots[0]].set(smallest).at[spots[1]].set(largest)


def shard_levels(own_key, dims, pieces, smallest, high):
    def one(position, shards_of):
        steps = jax.random.uniform(jax.random.fold_in(jax.random.fold_in(own_key, 6), position), (shards_of,), jnp.float32, smallest / len(pieces), high / len(pieces))
        return jnp.repeat(jnp.exp(steps), dims[position] // shards_of).reshape((-1,) + (1,) * (len(dims) - position - 1))

    level = one(*pieces[0])
    for cut in pieces[1:]:
        level = level * one(*cut)
    return level


def centred(stream_key, dims, scale, reach, cuts=(), held_as=jnp.bfloat16):
    loudness = shard_levels(stream_key, dims, cuts, -0.22, 0.18) if cuts else 1.0
    result = jax.random.normal(stream_key, dims, jnp.float32) * scale * loudness
    return jnp.minimum(jnp.maximum(result, -reach), reach).astype(held_as)


def setup_inputs(seed: int = 0) -> dict:
    keys = jax.random.split(jax.random.key(seed), 9)
    tokens = draw_tokens(jax.random.fold_in(keys[8], 71), 0)
    norm_gain = jnp.clip(1.0 + 0.18 * jax.random.normal(keys[1], (D,), jnp.float32), 0.1, 1.9)
    gate_weight = centred(keys[2], (D, FF), (D // 2) ** -0.5, 0.09375, ((1, 128),))
    up_weight = centred(keys[3], (D, FF), (D // 2) ** -0.5, 0.09375, ((1, 128),))
    down_weight = centred(keys[4], (FF, D), (FF // 2) ** -0.5, 0.046875, ((0, 128),))
    gate_mask = draw_gate_mask(jax.random.fold_in(keys[8], 71), 0)
    up_mask = draw_up_mask(jax.random.fold_in(keys[8], 71), 0)
    down_mask = with_ends((jax.random.randint(keys[7], (FB, RB), 0, 2) < 1).astype(jnp.int32), jax.random.fold_in(keys[7], 1), 0, 1)
    return dict(tokens=tokens, norm_gain=norm_gain, gate_weight=gate_weight, up_weight=up_weight, down_weight=down_weight, gate_mask=gate_mask, up_mask=up_mask, down_mask=down_mask)


def mask_blocks(weight, flags):
    height, width = weight.shape
    down_n = flags.shape[0]
    across_n = flags.shape[1]
    shaped = weight.reshape(down_n, height // down_n, across_n, width // across_n)
    return (shaped * flags.astype(weight.dtype)[:, None, :, None]).reshape(height, width)

def reference(tokens, norm_gain, gate_weight, up_weight, down_weight, gate_mask, up_mask, down_mask):
    wide_tok = tokens.astype(jnp.float32)
    scale_inv = lax.rsqrt(lax.optimization_barrier(jnp.mean(wide_tok * wide_tok, axis=-1, keepdims=True)) + 1e-05)
    normed = (wide_tok * scale_inv * norm_gain.astype(jnp.float32)).astype(jnp.bfloat16)
    flag_cols = PANEL // BLOCK

    def one_panel(index, total):
        panel_at = jnp.asarray(index).astype(jnp.int32) * PANEL
        flag_at = jnp.asarray(index).astype(jnp.int32) * flag_cols
        gate_part = mask_blocks(lax.dynamic_slice_in_dim(gate_weight, panel_at, PANEL, 1), lax.dynamic_slice_in_dim(gate_mask, flag_at, flag_cols, 1))
        up_part = mask_blocks(lax.dynamic_slice_in_dim(up_weight, panel_at, PANEL, 1), lax.dynamic_slice_in_dim(up_mask, flag_at, flag_cols, 1))
        down_part = mask_blocks(lax.dynamic_slice_in_dim(down_weight, panel_at, PANEL, 0), lax.dynamic_slice_in_dim(down_mask, flag_at, flag_cols, 0))
        gate = jnp.dot(normed, gate_part, preferred_element_type=jnp.float32)
        up_val = jnp.dot(normed, up_part, preferred_element_type=jnp.float32)
        hidden = (jax.nn.silu(gate) * up_val).astype(jnp.bfloat16)
        return total + jnp.dot(hidden, down_part, preferred_element_type=jnp.float32)
    start_sum = jnp.zeros((tokens.shape[0], tokens.shape[1]), jnp.float32)
    total = lax.fori_loop(0, FF // PANEL, one_panel, start_sum)
    return total.astype(jnp.bfloat16)
```

```python
import jax
import jax.numpy as jnp
from jax import lax
from jax.sharding import PartitionSpec as P

BLK_AXES = {"z": (16, 8), "xh": (8, 2), "y": (2, 4), "c": (1, 2)}
CANON = ("c", "z", "y", "xh")
AG_ORDER = ("xh", "y", "z", "c")
RS_ORDER = ("c", "z", "y", "xh")


def mask_blocks(weight, flags):
    height, width = weight.shape
    down_n = flags.shape[0]
    across_n = flags.shape[1]
    shaped = weight.reshape(down_n, height // down_n, across_n, width // across_n)
    return (shaped * flags.astype(weight.dtype)[:, None, :, None]).reshape(height, width)


def _perm(axis, k, size):
    stride, n = BLK_AXES[axis]
    pairs = []
    for i in range(size):
        coord = (i // stride) % n
        pairs.append((i, i + ((coord + k) % n - coord) * stride))
    return pairs


def _ag_stage(block, axis, size):
    _, n = BLK_AXES[axis]
    m_plus = n // 2
    m_minus = n - 1 - m_plus
    got = [None] * n
    got[0] = block
    cur = block
    for s in range(m_plus):
        cur = lax.ppermute(cur, "blk", _perm(axis, 1, size))
        got[n - s - 1] = cur
    cur = block
    for s in range(m_minus):
        cur = lax.ppermute(cur, "blk", _perm(axis, -1, size))
        got[s + 1] = cur
    return jnp.stack(got)


def _rs_stage(x, dim, axis, size):
    _, n = BLK_AXES[axis]
    m_plus = n // 2
    m_minus = n - 1 - m_plus

    def take(j):
        return lax.index_in_dim(x, j % n, axis=dim, keepdims=False)

    total = take(0)
    buf = take(m_plus)
    for s in range(m_plus):
        recv = lax.ppermute(buf, "blk", _perm(axis, 1, size))
        if s < m_plus - 1:
            buf = recv + take(m_plus - s - 1)
        else:
            total = total + recv
    if m_minus:
        buf = take(n - m_minus)
        for s in range(m_minus):
            recv = lax.ppermute(buf, "blk", _perm(axis, -1, size))
            if s < m_minus - 1:
                buf = recv + take(n - m_minus + s + 1)
            else:
                total = total + recv
    return total


def gather_tokens(normed, size):
    cur = normed
    for axis in AG_ORDER:
        cur = _ag_stage(cur, axis, size)
    names = list(reversed(AG_ORDER))
    cur = jnp.transpose(cur, [names.index(a) for a in CANON] + [len(names), len(names) + 1])
    return cur.reshape(-1, normed.shape[-1])


def scatter_sums(partial, t):
    size = 1
    for a in CANON:
        size *= BLK_AXES[a][1]
    x = partial.reshape(tuple(BLK_AXES[a][1] for a in CANON) + (t, partial.shape[-1]))
    names = list(CANON)
    for axis in RS_ORDER:
        d = names.index(axis)
        x = _rs_stage(x, d, axis, size)
        names.pop(d)
    return x


def local(tokens, norm_gain, gate_weight, up_weight, down_weight, gate_mask, up_mask, down_mask):
    size = 1
    for a in CANON:
        size *= BLK_AXES[a][1]
    wide_tok = tokens.astype(jnp.float32)
    scale_inv = lax.rsqrt(jnp.mean(wide_tok * wide_tok, axis=-1, keepdims=True) + 1e-05)
    normed = (wide_tok * scale_inv * norm_gain).astype(jnp.bfloat16)
    gate_kept = mask_blocks(gate_weight, gate_mask)
    up_kept = mask_blocks(up_weight, up_mask)
    down_kept = mask_blocks(down_weight, down_mask)
    piece = gather_tokens(normed, size)
    gate = jnp.dot(piece, gate_kept, preferred_element_type=jnp.float32)
    up_val = jnp.dot(piece, up_kept, preferred_element_type=jnp.float32)
    hidden = (jax.nn.silu(gate) * up_val).astype(jnp.bfloat16)
    partial = jnp.dot(hidden, down_kept, preferred_element_type=jnp.float32)
    summed = scatter_sums(partial, tokens.shape[0])
    return summed.astype(jnp.bfloat16)


def solution(mesh):
    assert mesh.shape["blk"] == 128
    return jax.shard_map(
        local,
        mesh=mesh,
        in_specs=(
            P(("blk", "rows"), None),
            P(),
            P(None, "blk"),
            P(None, "blk"),
            P("blk", None),
            P(None, "blk"),
            P(None, "blk"),
            P("blk", None),
        ),
        out_specs=P(("blk", "rows"), None),
        check_vma=False,
    )
```

```python
import jax
import jax.numpy as jnp
from jax import lax
from jax.sharding import PartitionSpec as P

BLK_AXES = {"z": (16, 8), "xh": (8, 2), "y": (2, 4), "c": (1, 2)}
PARTS = (
    (32, ("xh", "y", "z", "c"), ("c", "z", "y", "xh")),
    (32, ("xh", "z", "y", "c"), ("c", "y", "z", "xh")),
)


def mask_blocks(weight, flags):
    height, width = weight.shape
    down_n = flags.shape[0]
    across_n = flags.shape[1]
    shaped = weight.reshape(down_n, height // down_n, across_n, width // across_n)
    return (shaped * flags.astype(weight.dtype)[:, None, :, None]).reshape(height, width)


def _perm(axis, k, size):
    stride, n = BLK_AXES[axis]
    pairs = []
    for i in range(size):
        coord = (i // stride) % n
        pairs.append((i, i + ((coord + k) % n - coord) * stride))
    return pairs


def _ag_stage(block, axis, size):
    _, n = BLK_AXES[axis]
    m_plus = n // 2
    m_minus = n - 1 - m_plus
    got = [None] * n
    got[0] = block
    cur = block
    for s in range(m_plus):
        cur = lax.ppermute(cur, "blk", _perm(axis, 1, size))
        got[n - s - 1] = cur
    cur = block
    for s in range(m_minus):
        cur = lax.ppermute(cur, "blk", _perm(axis, -1, size))
        got[s + 1] = cur
    return jnp.concatenate(got, axis=0)


def _rs_stage(x, axis, size):
    _, n = BLK_AXES[axis]
    r = x.shape[0] // n
    m_plus = n // 2
    m_minus = n - 1 - m_plus

    def take(j):
        return lax.slice_in_dim(x, (j % n) * r, (j % n + 1) * r, axis=0)

    total = take(0)
    buf = take(m_plus)
    for s in range(m_plus):
        recv = lax.ppermute(buf, "blk", _perm(axis, 1, size))
        if s < m_plus - 1:
            buf = recv + take(m_plus - s - 1)
        else:
            total = total + recv
    if m_minus:
        buf = take(n - m_minus)
        for s in range(m_minus):
            recv = lax.ppermute(buf, "blk", _perm(axis, -1, size))
            if s < m_minus - 1:
                buf = recv + take(n - m_minus + s + 1)
            else:
                total = total + recv
    return total


def _reorder_rows(x, src, dst, t):
    sizes = tuple(BLK_AXES[a][1] for a in src) + (t,)
    y = x.reshape(sizes + x.shape[1:])
    perm = [src.index(a) for a in dst] + [len(src)] + [len(src) + 1 + i for i in range(x.ndim - 1)]
    return jnp.transpose(y, perm).reshape(x.shape)


def local(tokens, norm_gain, gate_weight, up_weight, down_weight, gate_mask, up_mask, down_mask):
    size = 1
    for a in BLK_AXES:
        size *= BLK_AXES[a][1]
    t = tokens.shape[0]
    wide_tok = tokens.astype(jnp.float32)
    scale_inv = lax.rsqrt(jnp.mean(wide_tok * wide_tok, axis=-1, keepdims=True) + 1e-05)
    normed = (wide_tok * scale_inv * norm_gain).astype(jnp.bfloat16)
    gate_kept = mask_blocks(gate_weight, gate_mask)
    up_kept = mask_blocks(up_weight, up_mask)
    down_kept = mask_blocks(down_weight, down_mask)

    base = tuple(reversed(PARTS[0][1]))
    gate = None
    up_val = None
    lo = 0
    for groups, ag_order, _ in PARTS:
        hi = lo + groups * 128
        piece = normed[:, lo:hi]
        for axis in ag_order:
            piece = _ag_stage(piece, axis, size)
        nest = tuple(reversed(ag_order))
        g = jnp.dot(piece, gate_kept[lo:hi], preferred_element_type=jnp.float32)
        u = jnp.dot(piece, up_kept[lo:hi], preferred_element_type=jnp.float32)
        if nest != base:
            g = _reorder_rows(g, nest, base, t)
            u = _reorder_rows(u, nest, base, t)
        gate = g if gate is None else gate + g
        up_val = u if up_val is None else up_val + u
        lo = hi
    hidden = (jax.nn.silu(gate) * up_val).astype(jnp.bfloat16)

    outs = []
    lo = 0
    for groups, _, rs_order in PARTS:
        hi = lo + groups * 128
        h = hidden if rs_order == base else _reorder_rows(hidden, base, rs_order, t)
        x = jnp.dot(h, down_kept[:, lo:hi], preferred_element_type=jnp.float32)
        for axis in rs_order:
            x = _rs_stage(x, axis, size)
        outs.append(x)
        lo = hi
    summed = jnp.concatenate(outs, axis=1) if len(outs) > 1 else outs[0]
    return summed.astype(jnp.bfloat16)


def solution(mesh):
    assert mesh.shape["blk"] == 128
    return jax.shard_map(
        local,
        mesh=mesh,
        in_specs=(
            P(("blk", "rows"), None),
            P(),
            P(None, "blk"),
            P(None, "blk"),
            P("blk", None),
            P(None, "blk"),
            P(None, "blk"),
            P("blk", None),
        ),
        out_specs=P(("blk", "rows"), None),
        check_vma=False,
    )
```

```python
import jax
import jax.numpy as jnp
from jax import lax
from jax.sharding import PartitionSpec as P

BLK_AXES = {"z": (16, 8), "xh": (8, 2), "y": (2, 4), "c": (1, 2)}
AG_ORDER = ("xh", "y", "z", "c")
PARTS = (
    (32, ("c", "z", "y", "xh")),
    (32, ("c", "y", "z", "xh")),
)


def mask_blocks(weight, flags):
    height, width = weight.shape
    down_n = flags.shape[0]
    across_n = flags.shape[1]
    cols = jnp.repeat(flags.astype(weight.dtype), width // across_n, axis=1)
    shaped = weight.reshape(down_n, height // down_n, width)
    return (shaped * cols[:, None, :]).reshape(height, width)


def _perm(axis, k, size):
    stride, n = BLK_AXES[axis]
    pairs = []
    for i in range(size):
        coord = (i // stride) % n
        pairs.append((i, i + ((coord + k) % n - coord) * stride))
    return pairs


def _ag_stage(block, axis, size):
    _, n = BLK_AXES[axis]
    m_plus = n // 2
    m_minus = n - 1 - m_plus
    got = [None] * n
    got[0] = block
    cur = block
    for s in range(m_plus):
        cur = lax.ppermute(cur, "blk", _perm(axis, 1, size))
        got[n - s - 1] = cur
    cur = block
    for s in range(m_minus):
        cur = lax.ppermute(cur, "blk", _perm(axis, -1, size))
        got[s + 1] = cur
    return jnp.concatenate(got, axis=0)


def _rs_stage(x, axis, size):
    _, n = BLK_AXES[axis]
    r = x.shape[0] // n
    m_plus = n // 2
    m_minus = n - 1 - m_plus

    def take(j):
        return lax.slice_in_dim(x, (j % n) * r, (j % n + 1) * r, axis=0)

    total = take(0)
    buf = take(m_plus)
    for s in range(m_plus):
        recv = lax.ppermute(buf, "blk", _perm(axis, 1, size))
        if s < m_plus - 1:
            buf = recv + take(m_plus - s - 1)
        else:
            total = total + recv
    if m_minus:
        buf = take(n - m_minus)
        for s in range(m_minus):
            recv = lax.ppermute(buf, "blk", _perm(axis, -1, size))
            if s < m_minus - 1:
                buf = recv + take(n - m_minus + s + 1)
            else:
                total = total + recv
    return total


def _reorder_rows(x, src, dst, t):
    sizes = tuple(BLK_AXES[a][1] for a in src) + (t,)
    y = x.reshape(sizes + x.shape[1:])
    perm = [src.index(a) for a in dst] + [len(src)] + [len(src) + 1 + i for i in range(x.ndim - 1)]
    return jnp.transpose(y, perm).reshape(x.shape)


def local(tokens, norm_gain, gate_weight, up_weight, down_weight, gate_mask, up_mask, down_mask):
    size = 1
    for a in BLK_AXES:
        size *= BLK_AXES[a][1]
    t = tokens.shape[0]
    wide_tok = tokens.astype(jnp.float32)
    scale_inv = lax.rsqrt(jnp.mean(wide_tok * wide_tok, axis=-1, keepdims=True) + 1e-05)
    normed = (wide_tok * scale_inv * norm_gain).astype(jnp.bfloat16)
    gate_kept = mask_blocks(gate_weight, gate_mask)
    up_kept = mask_blocks(up_weight, up_mask)
    down_kept = mask_blocks(down_weight, down_mask)

    base = tuple(reversed(AG_ORDER))
    piece = normed
    for axis in AG_ORDER:
        piece = _ag_stage(piece, axis, size)
    gate = jnp.dot(piece, gate_kept, preferred_element_type=jnp.float32)
    up_val = jnp.dot(piece, up_kept, preferred_element_type=jnp.float32)
    hidden = (jax.nn.silu(gate) * up_val).astype(jnp.bfloat16)

    outs = []
    lo = 0
    for groups, rs_order in PARTS:
        hi = lo + groups * 128
        h = hidden if rs_order == base else _reorder_rows(hidden, base, rs_order, t)
        x = jnp.dot(h, down_kept[:, lo:hi], preferred_element_type=jnp.float32)
        for axis in rs_order:
            x = _rs_stage(x, axis, size)
        outs.append(x)
        lo = hi
    summed = jnp.concatenate(outs, axis=1) if len(outs) > 1 else outs[0]
    return summed.astype(jnp.bfloat16)


def solution(mesh):
    assert mesh.shape["blk"] == 128
    return jax.shard_map(
        local,
        mesh=mesh,
        in_specs=(
            P(("blk", "rows"), None),
            P(),
            P(None, "blk"),
            P(None, "blk"),
            P("blk", None),
            P(None, "blk"),
            P(None, "blk"),
            P("blk", None),
        ),
        out_specs=P(("blk", "rows"), None),
        check_vma=False,
    )
```

```python
import jax
import jax.numpy as jnp
from jax import lax
from jax.sharding import PartitionSpec as P

BLK_AXES = {"z": (16, 8), "xh": (8, 2), "y": (2, 4), "c": (1, 2)}
AG_ORDER = ("xh", "y", "z", "c")
PARTS = (
    (32, ("c", "z", "y", "xh")),
    (32, ("c", "y", "z", "xh")),
)


def mask_blocks(weight, flags):
    height, width = weight.shape
    down_n = flags.shape[0]
    across_n = flags.shape[1]
    cols = jnp.repeat(flags.astype(weight.dtype), width // across_n, axis=1)
    shaped = weight.reshape(down_n, height // down_n, width)
    return (shaped * cols[:, None, :]).reshape(height, width)


def _perm(axis, k, size):
    stride, n = BLK_AXES[axis]
    pairs = []
    for i in range(size):
        coord = (i // stride) % n
        pairs.append((i, i + ((coord + k) % n - coord) * stride))
    return pairs


def _ag_stage(block, axis, size):
    _, n = BLK_AXES[axis]
    m_plus = n // 2
    m_minus = n - 1 - m_plus
    got = [None] * n
    got[0] = block
    cur = block
    for s in range(m_plus):
        cur = lax.ppermute(cur, "blk", _perm(axis, 1, size))
        got[n - s - 1] = cur
    cur = block
    for s in range(m_minus):
        cur = lax.ppermute(cur, "blk", _perm(axis, -1, size))
        got[s + 1] = cur
    return jnp.concatenate(got, axis=0)


def _rs_stage(x, axis, size):
    _, n = BLK_AXES[axis]
    r = x.shape[0] // n
    m_plus = n // 2
    m_minus = n - 1 - m_plus

    def take(j):
        return lax.slice_in_dim(x, (j % n) * r, (j % n + 1) * r, axis=0)

    total = take(0)
    buf = take(m_plus)
    for s in range(m_plus):
        recv = lax.ppermute(buf, "blk", _perm(axis, 1, size))
        if s < m_plus - 1:
            buf = recv + take(m_plus - s - 1)
        else:
            total = total + recv
    if m_minus:
        buf = take(n - m_minus)
        for s in range(m_minus):
            recv = lax.ppermute(buf, "blk", _perm(axis, -1, size))
            if s < m_minus - 1:
                buf = recv + take(n - m_minus + s + 1)
            else:
                total = total + recv
    return total


def _reorder_rows(x, src, dst, t):
    sizes = tuple(BLK_AXES[a][1] for a in src) + (t,)
    y = x.reshape(sizes + x.shape[1:])
    perm = [src.index(a) for a in dst] + [len(src)] + [len(src) + 1 + i for i in range(x.ndim - 1)]
    return jnp.transpose(y, perm).reshape(x.shape)


def local(tokens, norm_gain, gate_weight, up_weight, down_weight, gate_mask, up_mask, down_mask):
    size = 1
    for a in BLK_AXES:
        size *= BLK_AXES[a][1]
    t = tokens.shape[0]
    wide_tok = tokens.astype(jnp.float32)
    scale_inv = lax.rsqrt(jnp.mean(wide_tok * wide_tok, axis=-1, keepdims=True) + 1e-05)
    normed = (wide_tok * scale_inv * norm_gain).astype(jnp.bfloat16)
    gate_kept = mask_blocks(gate_weight, gate_mask)
    up_kept = mask_blocks(up_weight, up_mask)
    down_kept = mask_blocks(down_weight, down_mask)

    base = tuple(reversed(AG_ORDER))
    piece = normed
    for i, axis in enumerate(AG_ORDER[:-1]):
        piece = _ag_stage(piece, axis, size)
        if i == 0:
            piece, gate_kept, up_kept, down_kept = lax.optimization_barrier(
                (piece, gate_kept, up_kept, down_kept))
        else:
            piece = lax.optimization_barrier(piece)
    last = AG_ORDER[-1]
    _, n_last = BLK_AXES[last]
    assert n_last == 2
    blocks = [piece, lax.ppermute(piece, "blk", _perm(last, 1, size))]
    gate = jnp.concatenate(
        [jnp.dot(b, gate_kept, preferred_element_type=jnp.float32) for b in blocks], axis=0)
    up_val = jnp.concatenate(
        [jnp.dot(b, up_kept, preferred_element_type=jnp.float32) for b in blocks], axis=0)
    hidden = (jax.nn.silu(gate) * up_val).astype(jnp.bfloat16)

    outs = []
    lo = 0
    for groups, rs_order in PARTS:
        hi = lo + groups * 128
        h = hidden if rs_order == base else _reorder_rows(hidden, base, rs_order, t)
        x = jnp.dot(h, down_kept[:, lo:hi], preferred_element_type=jnp.float32)
        for axis in rs_order:
            x = _rs_stage(x, axis, size)
        outs.append(x)
        lo = hi
    summed = jnp.concatenate(outs, axis=1) if len(outs) > 1 else outs[0]
    return summed.astype(jnp.bfloat16)


def solution(mesh):
    assert mesh.shape["blk"] == 128
    return jax.shard_map(
        local,
        mesh=mesh,
        in_specs=(
            P(("blk", "rows"), None),
            P(),
            P(None, "blk"),
            P(None, "blk"),
            P("blk", None),
            P(None, "blk"),
            P(None, "blk"),
            P("blk", None),
        ),
        out_specs=P(("blk", "rows"), None),
        check_vma=False,
    )
```

```python
import jax
import jax.numpy as jnp
from jax import lax
from jax.sharding import PartitionSpec as P

BLK_AXES = {"z": (16, 8), "xh": (8, 2), "y": (2, 4), "c": (1, 2)}
AG_PARTS = (
    (32, ("xh", "y", "z", "c")),
    (32, ("xh", "z", "y", "c")),
)
PARTS = (
    (32, ("c", "z", "y", "xh")),
    (32, ("c", "y", "z", "xh")),
)


def mask_blocks(weight, flags):
    height, width = weight.shape
    down_n = flags.shape[0]
    across_n = flags.shape[1]
    cols = jnp.repeat(flags.astype(weight.dtype), width // across_n, axis=1)
    shaped = weight.reshape(down_n, height // down_n, width)
    return (shaped * cols[:, None, :]).reshape(height, width)


def _perm(axis, k, size):
    stride, n = BLK_AXES[axis]
    pairs = []
    for i in range(size):
        coord = (i // stride) % n
        pairs.append((i, i + ((coord + k) % n - coord) * stride))
    return pairs


def _ag_stage(block, axis, size):
    _, n = BLK_AXES[axis]
    m_plus = n // 2
    m_minus = n - 1 - m_plus
    got = [None] * n
    got[0] = block
    cur = block
    for s in range(m_plus):
        cur = lax.ppermute(cur, "blk", _perm(axis, 1, size))
        got[n - s - 1] = cur
    cur = block
    for s in range(m_minus):
        cur = lax.ppermute(cur, "blk", _perm(axis, -1, size))
        got[s + 1] = cur
    return jnp.concatenate(got, axis=0)


def _rs_stage(x, axis, size):
    _, n = BLK_AXES[axis]
    r = x.shape[0] // n
    m_plus = n // 2
    m_minus = n - 1 - m_plus

    def take(j):
        return lax.slice_in_dim(x, (j % n) * r, (j % n + 1) * r, axis=0)

    total = take(0)
    buf = take(m_plus)
    for s in range(m_plus):
        recv = lax.ppermute(buf, "blk", _perm(axis, 1, size))
        if s < m_plus - 1:
            buf = recv + take(m_plus - s - 1)
        else:
            total = total + recv
    if m_minus:
        buf = take(n - m_minus)
        for s in range(m_minus):
            recv = lax.ppermute(buf, "blk", _perm(axis, -1, size))
            if s < m_minus - 1:
                buf = recv + take(n - m_minus + s + 1)
            else:
                total = total + recv
    return total


def _reorder_rows(x, src, dst, t):
    sizes = tuple(BLK_AXES[a][1] for a in src) + (t,)
    y = x.reshape(sizes + x.shape[1:])
    perm = [src.index(a) for a in dst] + [len(src)] + [len(src) + 1 + i for i in range(x.ndim - 1)]
    return jnp.transpose(y, perm).reshape(x.shape)


def local(tokens, norm_gain, gate_weight, up_weight, down_weight, gate_mask, up_mask, down_mask):
    size = 1
    for a in BLK_AXES:
        size *= BLK_AXES[a][1]
    t = tokens.shape[0]
    wide_tok = tokens.astype(jnp.float32)
    scale_inv = lax.rsqrt(jnp.mean(wide_tok * wide_tok, axis=-1, keepdims=True) + 1e-05)
    normed = (wide_tok * scale_inv * norm_gain).astype(jnp.bfloat16)
    gate_kept = mask_blocks(gate_weight, gate_mask)
    up_kept = mask_blocks(up_weight, up_mask)
    down_kept = mask_blocks(down_weight, down_mask)

    base = tuple(reversed(AG_PARTS[0][1]))
    inner = base[1:]
    g_blocks = [None, None]
    u_blocks = [None, None]
    lo = 0
    for p, (groups, ag_order) in enumerate(AG_PARTS):
        hi = lo + groups * 128
        piece = normed[:, lo:hi]
        for i, axis in enumerate(ag_order[:-1]):
            piece = _ag_stage(piece, axis, size)
            if p == 0 and i == 0:
                piece, gate_kept, up_kept, down_kept = lax.optimization_barrier(
                    (piece, gate_kept, up_kept, down_kept))
            else:
                piece = lax.optimization_barrier(piece)
        last = ag_order[-1]
        assert last == base[0] and BLK_AXES[last][1] == 2
        nest = tuple(reversed(ag_order[:-1]))
        blocks = [piece, lax.ppermute(piece, "blk", _perm(last, 1, size))]
        for b, blk in enumerate(blocks):
            g = jnp.dot(blk, gate_kept[lo:hi], preferred_element_type=jnp.float32)
            u = jnp.dot(blk, up_kept[lo:hi], preferred_element_type=jnp.float32)
            if nest != inner:
                g = _reorder_rows(g, nest, inner, t)
                u = _reorder_rows(u, nest, inner, t)
            g_blocks[b] = g if g_blocks[b] is None else g_blocks[b] + g
            u_blocks[b] = u if u_blocks[b] is None else u_blocks[b] + u
        lo = hi
    gate = jnp.concatenate(g_blocks, axis=0)
    up_val = jnp.concatenate(u_blocks, axis=0)
    hidden = (jax.nn.silu(gate) * up_val).astype(jnp.bfloat16)

    outs = []
    lo = 0
    for groups, rs_order in PARTS:
        hi = lo + groups * 128
        h = hidden if rs_order == base else _reorder_rows(hidden, base, rs_order, t)
        x = jnp.dot(h, down_kept[:, lo:hi], preferred_element_type=jnp.float32)
        for axis in rs_order:
            x = _rs_stage(x, axis, size)
        outs.append(x)
        lo = hi
    summed = jnp.concatenate(outs, axis=1) if len(outs) > 1 else outs[0]
    return summed.astype(jnp.bfloat16)


def solution(mesh):
    assert mesh.shape["blk"] == 128
    return jax.shard_map(
        local,
        mesh=mesh,
        in_specs=(
            P(("blk", "rows"), None),
            P(),
            P(None, "blk"),
            P(None, "blk"),
            P("blk", None),
            P(None, "blk"),
            P(None, "blk"),
            P("blk", None),
        ),
        out_specs=P(("blk", "rows"), None),
        check_vma=False,
    )
```

```python
import jax
import jax.numpy as jnp
from jax import lax
from jax.sharding import PartitionSpec as P

BLK_AXES = {"z": (16, 8), "xh": (8, 2), "y": (2, 4), "c": (1, 2)}
AG_ORDER = (("y", "xh"), "z", "c")
PARTS = (
    (32, ("c", "z", ("y", "xh"))),
    (32, ("c", "y", "z", "xh")),
)


def mask_blocks(weight, flags):
    height, width = weight.shape
    down_n = flags.shape[0]
    across_n = flags.shape[1]
    cols = jnp.repeat(flags.astype(weight.dtype), width // across_n, axis=1)
    shaped = weight.reshape(down_n, height // down_n, width)
    return (shaped * cols[:, None, :]).reshape(height, width)


def _perm(axis, k, size):
    stride, n = BLK_AXES[axis]
    pairs = []
    for i in range(size):
        coord = (i // stride) % n
        pairs.append((i, i + ((coord + k) % n - coord) * stride))
    return pairs


def _perm_multi(offs, size):
    pairs = []
    for i in range(size):
        j = i
        for axis, k in offs.items():
            stride, n = BLK_AXES[axis]
            coord = (i // stride) % n
            j += ((coord + k) % n - coord) * stride
        pairs.append((i, j))
    return pairs


def _offsets(group):
    out = [()]
    for axis in group:
        out = [o + (k,) for o in out for k in range(BLK_AXES[axis][1])]
    return out


def _ag_direct(block, group, size):
    got = []
    for o in _offsets(group):
        if not any(o):
            got.append(block)
            continue
        offs = {a: -k for a, k in zip(group, o)}
        got.append(lax.ppermute(block, "blk", _perm_multi(offs, size)))
    return jnp.concatenate(got, axis=0)


def _rs_direct(x, group, size):
    offsets = _offsets(group)
    r = x.shape[0] // len(offsets)
    total = None
    for idx, o in enumerate(offsets):
        part = lax.slice_in_dim(x, idx * r, (idx + 1) * r, axis=0)
        if any(o):
            part = lax.ppermute(part, "blk", _perm_multi(dict(zip(group, o)), size))
        total = part if total is None else total + part
    return total


def _ag_stage(block, axis, size):
    _, n = BLK_AXES[axis]
    m_plus = n // 2
    m_minus = n - 1 - m_plus
    got = [None] * n
    got[0] = block
    cur = block
    for s in range(m_plus):
        cur = lax.ppermute(cur, "blk", _perm(axis, 1, size))
        got[n - s - 1] = cur
    cur = block
    for s in range(m_minus):
        cur = lax.ppermute(cur, "blk", _perm(axis, -1, size))
        got[s + 1] = cur
    return jnp.concatenate(got, axis=0)


def _rs_stage(x, axis, size):
    _, n = BLK_AXES[axis]
    r = x.shape[0] // n
    m_plus = n // 2
    m_minus = n - 1 - m_plus

    def take(j):
        return lax.slice_in_dim(x, (j % n) * r, (j % n + 1) * r, axis=0)

    total = take(0)
    buf = take(m_plus)
    for s in range(m_plus):
        recv = lax.ppermute(buf, "blk", _perm(axis, 1, size))
        if s < m_plus - 1:
            buf = recv + take(m_plus - s - 1)
        else:
            total = total + recv
    if m_minus:
        buf = take(n - m_minus)
        for s in range(m_minus):
            recv = lax.ppermute(buf, "blk", _perm(axis, -1, size))
            if s < m_minus - 1:
                buf = recv + take(n - m_minus + s + 1)
            else:
                total = total + recv
    return total


def _flat(order):
    out = []
    for a in order:
        out.extend(a if isinstance(a, tuple) else (a,))
    return tuple(out)


def _reorder_rows(x, src, dst, t):
    sizes = tuple(BLK_AXES[a][1] for a in src) + (t,)
    y = x.reshape(sizes + x.shape[1:])
    perm = [src.index(a) for a in dst] + [len(src)] + [len(src) + 1 + i for i in range(x.ndim - 1)]
    return jnp.transpose(y, perm).reshape(x.shape)


def local(tokens, norm_gain, gate_weight, up_weight, down_weight, gate_mask, up_mask, down_mask):
    size = 1
    for a in BLK_AXES:
        size *= BLK_AXES[a][1]
    t = tokens.shape[0]
    wide_tok = tokens.astype(jnp.float32)
    scale_inv = lax.rsqrt(jnp.mean(wide_tok * wide_tok, axis=-1, keepdims=True) + 1e-05)
    normed = (wide_tok * scale_inv * norm_gain).astype(jnp.bfloat16)
    gate_kept = mask_blocks(gate_weight, gate_mask)
    up_kept = mask_blocks(up_weight, up_mask)
    down_kept = mask_blocks(down_weight, down_mask)

    base = _flat(tuple(reversed(AG_ORDER)))
    piece = normed
    for i, axis in enumerate(AG_ORDER[:-1]):
        if isinstance(axis, tuple):
            piece = _ag_direct(piece, axis, size)
        else:
            piece = _ag_stage(piece, axis, size)
        if i == 0:
            piece, gate_kept, up_kept, down_kept = lax.optimization_barrier(
                (piece, gate_kept, up_kept, down_kept))
        else:
            piece = lax.optimization_barrier(piece)
    last = AG_ORDER[-1]
    _, n_last = BLK_AXES[last]
    assert n_last == 2
    blocks = [piece, lax.ppermute(piece, "blk", _perm(last, 1, size))]
    gate = jnp.concatenate(
        [jnp.dot(b, gate_kept, preferred_element_type=jnp.float32) for b in blocks], axis=0)
    up_val = jnp.concatenate(
        [jnp.dot(b, up_kept, preferred_element_type=jnp.float32) for b in blocks], axis=0)
    hidden = (jax.nn.silu(gate) * up_val).astype(jnp.bfloat16)

    outs = []
    lo = 0
    for groups, rs_order in PARTS:
        hi = lo + groups * 128
        nest = _flat(rs_order)
        h = hidden if nest == base else _reorder_rows(hidden, base, nest, t)
        x = jnp.dot(h, down_kept[:, lo:hi], preferred_element_type=jnp.float32)
        for axis in rs_order:
            if isinstance(axis, tuple):
                x = _rs_direct(x, axis, size)
            else:
                x = _rs_stage(x, axis, size)
        outs.append(x)
        lo = hi
    summed = jnp.concatenate(outs, axis=1) if len(outs) > 1 else outs[0]
    return summed.astype(jnp.bfloat16)


def solution(mesh):
    assert mesh.shape["blk"] == 128
    return jax.shard_map(
        local,
        mesh=mesh,
        in_specs=(
            P(("blk", "rows"), None),
            P(),
            P(None, "blk"),
            P(None, "blk"),
            P("blk", None),
            P(None, "blk"),
            P(None, "blk"),
            P("blk", None),
        ),
        out_specs=P(("blk", "rows"), None),
        check_vma=False,
    )
```

```python
import jax
import jax.numpy as jnp
from jax import lax
from jax.sharding import PartitionSpec as P

BLK_AXES = {"z": (16, 8), "xh": (8, 2), "y": (2, 4), "c": (1, 2)}
AG_ORDER = ("xh", "y", "z", "c")
PARTS = (
    (32, ("c", "z", "y", "xh")),
    (32, ("c", "y", "z", "xh")),
)


def mask_blocks(weight, flags):
    height, width = weight.shape
    down_n = flags.shape[0]
    across_n = flags.shape[1]
    cols = jnp.repeat(flags.astype(weight.dtype), width // across_n, axis=1)
    shaped = weight.reshape(down_n, height // down_n, width)
    return (shaped * cols[:, None, :]).reshape(height, width)


def _perm(axis, k, size):
    stride, n = BLK_AXES[axis]
    cstride = BLK_AXES["c"][0]
    pairs = []
    for i in range(size):
        kk = k if (i // cstride) % 2 == 0 else -k
        coord = (i // stride) % n
        pairs.append((i, i + ((coord + kk) % n - coord) * stride))
    return pairs


def _ag_stage(block, axis, size):
    _, n = BLK_AXES[axis]
    m_plus = n // 2
    m_minus = n - 1 - m_plus
    got = [None] * n
    got[0] = block
    cur = block
    for s in range(m_plus):
        cur = lax.ppermute(cur, "blk", _perm(axis, 1, size))
        got[n - s - 1] = cur
    cur = block
    for s in range(m_minus):
        cur = lax.ppermute(cur, "blk", _perm(axis, -1, size))
        got[s + 1] = cur
    return jnp.concatenate(got, axis=0)


def _rs_stage(x, axis, size):
    _, n = BLK_AXES[axis]
    r = x.shape[0] // n
    m_plus = n // 2
    m_minus = n - 1 - m_plus

    def take(j):
        return lax.slice_in_dim(x, (j % n) * r, (j % n + 1) * r, axis=0)

    total = take(0)
    buf = take(m_plus)
    for s in range(m_plus):
        recv = lax.ppermute(buf, "blk", _perm(axis, 1, size))
        if s < m_plus - 1:
            buf = recv + take(m_plus - s - 1)
        else:
            total = total + recv
    if m_minus:
        buf = take(n - m_minus)
        for s in range(m_minus):
            recv = lax.ppermute(buf, "blk", _perm(axis, -1, size))
            if s < m_minus - 1:
                buf = recv + take(n - m_minus + s + 1)
            else:
                total = total + recv
    return total


def _reorder_rows(x, src, dst, t):
    sizes = tuple(BLK_AXES[a][1] for a in src) + (t,)
    y = x.reshape(sizes + x.shape[1:])
    perm = [src.index(a) for a in dst] + [len(src)] + [len(src) + 1 + i for i in range(x.ndim - 1)]
    return jnp.transpose(y, perm).reshape(x.shape)


def local(tokens, norm_gain, gate_weight, up_weight, down_weight, gate_mask, up_mask, down_mask):
    size = 1
    for a in BLK_AXES:
        size *= BLK_AXES[a][1]
    t = tokens.shape[0]
    wide_tok = tokens.astype(jnp.float32)
    scale_inv = lax.rsqrt(jnp.mean(wide_tok * wide_tok, axis=-1, keepdims=True) + 1e-05)
    normed = (wide_tok * scale_inv * norm_gain).astype(jnp.bfloat16)
    gate_kept = mask_blocks(gate_weight, gate_mask)
    up_kept = mask_blocks(up_weight, up_mask)
    down_kept = mask_blocks(down_weight, down_mask)

    base = tuple(reversed(AG_ORDER))
    piece = normed
    for i, axis in enumerate(AG_ORDER[:-1]):
        piece = _ag_stage(piece, axis, size)
        if i == 0:
            piece, gate_kept, up_kept, down_kept = lax.optimization_barrier(
                (piece, gate_kept, up_kept, down_kept))
        else:
            piece = lax.optimization_barrier(piece)
    last = AG_ORDER[-1]
    _, n_last = BLK_AXES[last]
    assert n_last == 2
    blocks = [piece, lax.ppermute(piece, "blk", _perm(last, 1, size))]
    gate = jnp.concatenate(
        [jnp.dot(b, gate_kept, preferred_element_type=jnp.float32) for b in blocks], axis=0)
    up_val = jnp.concatenate(
        [jnp.dot(b, up_kept, preferred_element_type=jnp.float32) for b in blocks], axis=0)
    hidden = (jax.nn.silu(gate) * up_val).astype(jnp.bfloat16)

    outs = []
    lo = 0
    for groups, rs_order in PARTS:
        hi = lo + groups * 128
        h = hidden if rs_order == base else _reorder_rows(hidden, base, rs_order, t)
        x = jnp.dot(h, down_kept[:, lo:hi], preferred_element_type=jnp.float32)
        for axis in rs_order:
            x = _rs_stage(x, axis, size)
        outs.append(x)
        lo = hi
    summed = jnp.concatenate(outs, axis=1) if len(outs) > 1 else outs[0]
    return summed.astype(jnp.bfloat16)


def solution(mesh):
    assert mesh.shape["blk"] == 128
    return jax.shard_map(
        local,
        mesh=mesh,
        in_specs=(
            P(("blk", "rows"), None),
            P(),
            P(None, "blk"),
            P(None, "blk"),
            P("blk", None),
            P(None, "blk"),
            P(None, "blk"),
            P("blk", None),
        ),
        out_specs=P(("blk", "rows"), None),
        check_vma=False,
    )
```

```python
import jax
import jax.numpy as jnp
from jax import lax
from jax.sharding import PartitionSpec as P

BLK_AXES = {"z": (16, 8), "xh": (8, 2), "y": (2, 4), "c": (1, 2)}
AG_ORDER = ("xh", "y", "z", "c")
PARTS = (
    (32, ("c", "z", "y", "xh")),
    (32, ("c", "y", "z", "xh")),
)


def mask_blocks(weight, flags):
    height, width = weight.shape
    down_n = flags.shape[0]
    across_n = flags.shape[1]
    cols = jnp.repeat(flags.astype(weight.dtype), width // across_n, axis=1)
    shaped = weight.reshape(down_n, height // down_n, width)
    return (shaped * cols[:, None, :]).reshape(height, width)


def _perm(axis, k, size):
    stride, n = BLK_AXES[axis]
    cstride = BLK_AXES["c"][0]
    pairs = []
    for i in range(size):
        kk = k if (i // cstride) % 2 == 0 else -k
        coord = (i // stride) % n
        pairs.append((i, i + ((coord + kk) % n - coord) * stride))
    return pairs


def _ag_stage(block, axis, size):
    _, n = BLK_AXES[axis]
    m_plus = n // 2
    m_minus = n - 1 - m_plus
    got = [None] * n
    got[0] = block
    cur = block
    for s in range(m_plus):
        cur = lax.ppermute(cur, "blk", _perm(axis, 1, size))
        got[n - s - 1] = cur
    cur = block
    for s in range(m_minus):
        cur = lax.ppermute(cur, "blk", _perm(axis, -1, size))
        got[s + 1] = cur
    return jnp.concatenate(got, axis=0)


def _rs_stage(x, axis, size):
    _, n = BLK_AXES[axis]
    r = x.shape[0] // n
    m_plus = n // 2
    m_minus = n - 1 - m_plus

    def take(j):
        return lax.slice_in_dim(x, (j % n) * r, (j % n + 1) * r, axis=0)

    total = take(0)
    buf = take(m_plus)
    for s in range(m_plus):
        recv = lax.ppermute(buf, "blk", _perm(axis, 1, size))
        if s < m_plus - 1:
            buf = recv + take(m_plus - s - 1)
        else:
            total = total + recv
    if m_minus:
        buf = take(n - m_minus)
        for s in range(m_minus):
            recv = lax.ppermute(buf, "blk", _perm(axis, -1, size))
            if s < m_minus - 1:
                buf = recv + take(n - m_minus + s + 1)
            else:
                total = total + recv
    return total


def _reorder_rows(x, src, dst, t):
    sizes = tuple(BLK_AXES[a][1] for a in src) + (t,)
    y = x.reshape(sizes + x.shape[1:])
    perm = [src.index(a) for a in dst] + [len(src)] + [len(src) + 1 + i for i in range(x.ndim - 1)]
    return jnp.transpose(y, perm).reshape(x.shape)


def local(tokens, norm_gain, gate_weight, up_weight, down_weight, gate_mask, up_mask, down_mask):
    size = 1
    for a in BLK_AXES:
        size *= BLK_AXES[a][1]
    t = tokens.shape[0]
    wide_tok = tokens.astype(jnp.float32)
    scale_inv = lax.rsqrt(jnp.mean(wide_tok * wide_tok, axis=-1, keepdims=True) + 1e-05)
    normed = (wide_tok * scale_inv * norm_gain).astype(jnp.bfloat16)
    gate_kept = mask_blocks(gate_weight, gate_mask)
    up_kept = mask_blocks(up_weight, up_mask)
    down_kept = mask_blocks(down_weight, down_mask)

    base = tuple(reversed(AG_ORDER))
    piece = normed
    kept = [gate_kept, up_kept, down_kept]
    for i, axis in enumerate(AG_ORDER[:-1]):
        piece = _ag_stage(piece, axis, size)
        piece, kept[i] = lax.optimization_barrier((piece, kept[i]))
    gate_kept, up_kept, down_kept = kept
    last = AG_ORDER[-1]
    _, n_last = BLK_AXES[last]
    assert n_last == 2
    blocks = [piece, lax.ppermute(piece, "blk", _perm(last, 1, size))]
    gate = jnp.concatenate(
        [jnp.dot(b, gate_kept, preferred_element_type=jnp.float32) for b in blocks], axis=0)
    up_val = jnp.concatenate(
        [jnp.dot(b, up_kept, preferred_element_type=jnp.float32) for b in blocks], axis=0)
    hidden = (jax.nn.silu(gate) * up_val).astype(jnp.bfloat16)

    outs = []
    lo = 0
    for groups, rs_order in PARTS:
        hi = lo + groups * 128
        h = hidden if rs_order == base else _reorder_rows(hidden, base, rs_order, t)
        x = jnp.dot(h, down_kept[:, lo:hi], preferred_element_type=jnp.float32)
        for axis in rs_order:
            x = _rs_stage(x, axis, size)
        outs.append(x)
        lo = hi
    summed = jnp.concatenate(outs, axis=1) if len(outs) > 1 else outs[0]
    return summed.astype(jnp.bfloat16)


def solution(mesh):
    assert mesh.shape["blk"] == 128
    return jax.shard_map(
        local,
        mesh=mesh,
        in_specs=(
            P(("blk", "rows"), None),
            P(),
            P(None, "blk"),
            P(None, "blk"),
            P("blk", None),
            P(None, "blk"),
            P(None, "blk"),
            P("blk", None),
        ),
        out_specs=P(("blk", "rows"), None),
        check_vma=False,
    )
```

```python
import jax
import jax.numpy as jnp
from jax import lax
from jax.sharding import PartitionSpec as P

BLK_AXES = {"z": (16, 8), "xh": (8, 2), "y": (2, 4), "c": (1, 2)}
AG_ORDER = ("xh", "y", "z")
PARTS = (
    (32, ("z", "y", "xh")),
    (32, ("y", "z", "xh")),
)


def mask_blocks(weight, flags):
    height, width = weight.shape
    down_n = flags.shape[0]
    across_n = flags.shape[1]
    cols = jnp.repeat(flags.astype(weight.dtype), width // across_n, axis=1)
    shaped = weight.reshape(down_n, height // down_n, width)
    return (shaped * cols[:, None, :]).reshape(height, width)


def _perm(axis, k, size):
    stride, n = BLK_AXES[axis]
    cstride = BLK_AXES["c"][0]
    pairs = []
    for i in range(size):
        kk = k if (i // cstride) % 2 == 0 else -k
        coord = (i // stride) % n
        pairs.append((i, i + ((coord + kk) % n - coord) * stride))
    return pairs


def _ag_stage(block, axis, size):
    _, n = BLK_AXES[axis]
    m_plus = n // 2
    m_minus = n - 1 - m_plus
    got = [None] * n
    got[0] = block
    cur = block
    for s in range(m_plus):
        cur = lax.ppermute(cur, "blk", _perm(axis, 1, size))
        got[n - s - 1] = cur
    cur = block
    for s in range(m_minus):
        cur = lax.ppermute(cur, "blk", _perm(axis, -1, size))
        got[s + 1] = cur
    return jnp.concatenate(got, axis=0)


def _rs_stage(x, axis, size):
    _, n = BLK_AXES[axis]
    r = x.shape[0] // n
    m_plus = n // 2
    m_minus = n - 1 - m_plus

    def take(j):
        return lax.slice_in_dim(x, (j % n) * r, (j % n + 1) * r, axis=0)

    total = take(0)
    buf = take(m_plus)
    for s in range(m_plus):
        recv = lax.ppermute(buf, "blk", _perm(axis, 1, size))
        if s < m_plus - 1:
            buf = recv + take(m_plus - s - 1)
        else:
            total = total + recv
    if m_minus:
        buf = take(n - m_minus)
        for s in range(m_minus):
            recv = lax.ppermute(buf, "blk", _perm(axis, -1, size))
            if s < m_minus - 1:
                buf = recv + take(n - m_minus + s + 1)
            else:
                total = total + recv
    return total


def _reorder_rows(x, src, dst, t):
    sizes = tuple(BLK_AXES[a][1] for a in src) + (t,)
    y = x.reshape(sizes + x.shape[1:])
    perm = [src.index(a) for a in dst] + [len(src)] + [len(src) + 1 + i for i in range(x.ndim - 1)]
    return jnp.transpose(y, perm).reshape(x.shape)


def local(tokens, norm_gain, gate_weight, up_weight, down_weight, gate_mask, up_mask, down_mask):
    size = 1
    for a in BLK_AXES:
        size *= BLK_AXES[a][1]
    t = tokens.shape[0]
    wide_tok = tokens.astype(jnp.float32)
    scale_inv = lax.rsqrt(jnp.mean(wide_tok * wide_tok, axis=-1, keepdims=True) + 1e-05)
    normed = (wide_tok * scale_inv * norm_gain).astype(jnp.bfloat16)
    gate_kept = mask_blocks(gate_weight, gate_mask)
    up_kept = mask_blocks(up_weight, up_mask)
    down_kept = mask_blocks(down_weight, down_mask)

    base = tuple(reversed(AG_ORDER))
    piece = normed
    tied = [(gate_kept,), (up_kept, down_kept), ()]
    kept = []
    for i, axis in enumerate(AG_ORDER):
        piece = _ag_stage(piece, axis, size)
        piece, done = lax.optimization_barrier((piece, tied[i]))
        kept.extend(done)
    swap = _perm("c", 1, size)
    weights = [(w, lax.ppermute(w, "blk", swap)) for w in kept]
    hidden = []
    for g_w, u_w in zip(weights[0], weights[1]):
        gate = jnp.dot(piece, g_w, preferred_element_type=jnp.float32)
        up_val = jnp.dot(piece, u_w, preferred_element_type=jnp.float32)
        hidden.append((jax.nn.silu(gate) * up_val).astype(jnp.bfloat16))

    outs = []
    lo = 0
    for groups, rs_order in PARTS:
        hi = lo + groups * 128
        x = None
        for h, d_w in zip(hidden, weights[2]):
            h = h if rs_order == base else _reorder_rows(h, base, rs_order, t)
            y = jnp.dot(h, d_w[:, lo:hi], preferred_element_type=jnp.float32)
            x = y if x is None else x + y
        for axis in rs_order:
            x = _rs_stage(x, axis, size)
        outs.append(x)
        lo = hi
    summed = jnp.concatenate(outs, axis=1) if len(outs) > 1 else outs[0]
    return summed.astype(jnp.bfloat16)


def solution(mesh):
    assert mesh.shape["blk"] == 128
    return jax.shard_map(
        local,
        mesh=mesh,
        in_specs=(
            P(("blk", "rows"), None),
            P(),
            P(None, "blk"),
            P(None, "blk"),
            P("blk", None),
            P(None, "blk"),
            P(None, "blk"),
            P("blk", None),
        ),
        out_specs=P(("blk", "rows"), None),
        check_vma=False,
    )
```

```python
import jax
import jax.numpy as jnp
from jax import lax
from jax.sharding import PartitionSpec as P

BLK_AXES = {"z": (16, 8), "xh": (8, 2), "y": (2, 4), "c": (1, 2)}
AG_ORDER = ("xh", "y", "z", "c")
PARTS = (
    (36, ("c", "z", "y", "xh")),
    (28, ("c", "y", "z", "xh")),
)


def mask_blocks(weight, flags):
    height, width = weight.shape
    down_n = flags.shape[0]
    across_n = flags.shape[1]
    cols = jnp.repeat(flags.astype(weight.dtype), width // across_n, axis=1)
    shaped = weight.reshape(down_n, height // down_n, width)
    return (shaped * cols[:, None, :]).reshape(height, width)


def _perm(axis, k, size):
    stride, n = BLK_AXES[axis]
    cstride = BLK_AXES["c"][0]
    pairs = []
    for i in range(size):
        kk = k if (i // cstride) % 2 == 0 else -k
        coord = (i // stride) % n
        pairs.append((i, i + ((coord + kk) % n - coord) * stride))
    return pairs


def _ag_stage(block, axis, size):
    _, n = BLK_AXES[axis]
    m_plus = n // 2
    m_minus = n - 1 - m_plus
    got = [None] * n
    got[0] = block
    cur = block
    for s in range(m_plus):
        cur = lax.ppermute(cur, "blk", _perm(axis, 1, size))
        got[n - s - 1] = cur
    cur = block
    for s in range(m_minus):
        cur = lax.ppermute(cur, "blk", _perm(axis, -1, size))
        got[s + 1] = cur
    return jnp.concatenate(got, axis=0)


def _rs_stage(x, axis, size):
    _, n = BLK_AXES[axis]
    r = x.shape[0] // n
    m_plus = n // 2
    m_minus = n - 1 - m_plus

    def take(j):
        return lax.slice_in_dim(x, (j % n) * r, (j % n + 1) * r, axis=0)

    total = take(0)
    buf = take(m_plus)
    for s in range(m_plus):
        recv = lax.ppermute(buf, "blk", _perm(axis, 1, size))
        if s < m_plus - 1:
            buf = recv + take(m_plus - s - 1)
        else:
            total = total + recv
    if m_minus:
        buf = take(n - m_minus)
        for s in range(m_minus):
            recv = lax.ppermute(buf, "blk", _perm(axis, -1, size))
            if s < m_minus - 1:
                buf = recv + take(n - m_minus + s + 1)
            else:
                total = total + recv
    return total


def _reorder_rows(x, src, dst, t):
    sizes = tuple(BLK_AXES[a][1] for a in src) + (t,)
    y = x.reshape(sizes + x.shape[1:])
    perm = [src.index(a) for a in dst] + [len(src)] + [len(src) + 1 + i for i in range(x.ndim - 1)]
    return jnp.transpose(y, perm).reshape(x.shape)


def local(tokens, norm_gain, gate_weight, up_weight, down_weight, gate_mask, up_mask, down_mask):
    size = 1
    for a in BLK_AXES:
        size *= BLK_AXES[a][1]
    t = tokens.shape[0]
    wide_tok = tokens.astype(jnp.float32)
    scale_inv = lax.rsqrt(jnp.mean(wide_tok * wide_tok, axis=-1, keepdims=True) + 1e-05)
    normed = (wide_tok * scale_inv * norm_gain).astype(jnp.bfloat16)
    gate_kept = mask_blocks(gate_weight, gate_mask)
    up_kept = mask_blocks(up_weight, up_mask)
    down_kept = mask_blocks(down_weight, down_mask)

    base = tuple(reversed(AG_ORDER))
    piece = normed
    kept = [gate_kept, up_kept, down_kept]
    for i, axis in enumerate(AG_ORDER[:-1]):
        piece = _ag_stage(piece, axis, size)
        piece, kept[i] = lax.optimization_barrier((piece, kept[i]))
    gate_kept, up_kept, down_kept = kept
    last = AG_ORDER[-1]
    _, n_last = BLK_AXES[last]
    assert n_last == 2
    blocks = [piece, lax.ppermute(piece, "blk", _perm(last, 1, size))]
    gate = jnp.concatenate(
        [jnp.dot(b, gate_kept, preferred_element_type=jnp.float32) for b in blocks], axis=0)
    up_val = jnp.concatenate(
        [jnp.dot(b, up_kept, preferred_element_type=jnp.float32) for b in blocks], axis=0)
    hidden = (jax.nn.silu(gate) * up_val).astype(jnp.bfloat16)

    outs = []
    lo = 0
    for groups, rs_order in PARTS:
        hi = lo + groups * 128
        h = hidden if rs_order == base else _reorder_rows(hidden, base, rs_order, t)
        x = jnp.dot(h, down_kept[:, lo:hi], preferred_element_type=jnp.float32)
        for axis in rs_order:
            x = _rs_stage(x, axis, size)
        outs.append(x)
        lo = hi
    summed = jnp.concatenate(outs, axis=1) if len(outs) > 1 else outs[0]
    return summed.astype(jnp.bfloat16)


def solution(mesh):
    assert mesh.shape["blk"] == 128
    return jax.shard_map(
        local,
        mesh=mesh,
        in_specs=(
            P(("blk", "rows"), None),
            P(),
            P(None, "blk"),
            P(None, "blk"),
            P("blk", None),
            P(None, "blk"),
            P(None, "blk"),
            P("blk", None),
        ),
        out_specs=P(("blk", "rows"), None),
        check_vma=False,
    )
```

```python
import jax
import jax.numpy as jnp
from jax import lax
from jax.sharding import PartitionSpec as P

BLK_AXES = {"z": (16, 8), "xh": (8, 2), "y": (2, 4), "c": (1, 2)}
AG_ORDER = ("xh", "y", "z", "c")
AG_DIRECT = ("y",)
PARTS = (
    (32, ("c", "z", "y", "xh"), ("y",)),
    (32, ("c", "y", "z", "xh"), ()),
)


def mask_blocks(weight, flags):
    height, width = weight.shape
    down_n = flags.shape[0]
    across_n = flags.shape[1]
    cols = jnp.repeat(flags.astype(weight.dtype), width // across_n, axis=1)
    shaped = weight.reshape(down_n, height // down_n, width)
    return (shaped * cols[:, None, :]).reshape(height, width)


def _perm(axis, k, size):
    stride, n = BLK_AXES[axis]
    cstride = BLK_AXES["c"][0]
    pairs = []
    for i in range(size):
        kk = k if (i // cstride) % 2 == 0 else -k
        coord = (i // stride) % n
        pairs.append((i, i + ((coord + kk) % n - coord) * stride))
    return pairs


def _ag_stage(block, axis, size):
    _, n = BLK_AXES[axis]
    m_plus = n // 2
    m_minus = n - 1 - m_plus
    got = [None] * n
    got[0] = block
    cur = block
    for s in range(m_plus):
        cur = lax.ppermute(cur, "blk", _perm(axis, 1, size))
        got[n - s - 1] = cur
    cur = block
    for s in range(m_minus):
        cur = lax.ppermute(cur, "blk", _perm(axis, -1, size))
        got[s + 1] = cur
    return jnp.concatenate(got, axis=0)


def _ag_direct(block, axis, size):
    _, n = BLK_AXES[axis]
    got = [block] + [lax.ppermute(block, "blk", _perm(axis, -o, size)) for o in range(1, n)]
    return jnp.concatenate(got, axis=0)


def _rs_direct(x, axis, size):
    _, n = BLK_AXES[axis]
    r = x.shape[0] // n
    total = lax.slice_in_dim(x, 0, r, axis=0)
    for o in range(1, n):
        part = lax.slice_in_dim(x, o * r, (o + 1) * r, axis=0)
        total = total + lax.ppermute(part, "blk", _perm(axis, o, size))
    return total


def _rs_stage(x, axis, size):
    _, n = BLK_AXES[axis]
    r = x.shape[0] // n
    m_plus = n // 2
    m_minus = n - 1 - m_plus

    def take(j):
        return lax.slice_in_dim(x, (j % n) * r, (j % n + 1) * r, axis=0)

    total = take(0)
    buf = take(m_plus)
    for s in range(m_plus):
        recv = lax.ppermute(buf, "blk", _perm(axis, 1, size))
        if s < m_plus - 1:
            buf = recv + take(m_plus - s - 1)
        else:
            total = total + recv
    if m_minus:
        buf = take(n - m_minus)
        for s in range(m_minus):
            recv = lax.ppermute(buf, "blk", _perm(axis, -1, size))
            if s < m_minus - 1:
                buf = recv + take(n - m_minus + s + 1)
            else:
                total = total + recv
    return total


def _reorder_rows(x, src, dst, t):
    sizes = tuple(BLK_AXES[a][1] for a in src) + (t,)
    y = x.reshape(sizes + x.shape[1:])
    perm = [src.index(a) for a in dst] + [len(src)] + [len(src) + 1 + i for i in range(x.ndim - 1)]
    return jnp.transpose(y, perm).reshape(x.shape)


def local(tokens, norm_gain, gate_weight, up_weight, down_weight, gate_mask, up_mask, down_mask):
    size = 1
    for a in BLK_AXES:
        size *= BLK_AXES[a][1]
    t = tokens.shape[0]
    wide_tok = tokens.astype(jnp.float32)
    scale_inv = lax.rsqrt(jnp.mean(wide_tok * wide_tok, axis=-1, keepdims=True) + 1e-05)
    normed = (wide_tok * scale_inv * norm_gain).astype(jnp.bfloat16)
    gate_kept = mask_blocks(gate_weight, gate_mask)
    up_kept = mask_blocks(up_weight, up_mask)
    down_kept = mask_blocks(down_weight, down_mask)

    base = tuple(reversed(AG_ORDER))
    piece = normed
    kept = [gate_kept, up_kept, down_kept]
    for i, axis in enumerate(AG_ORDER[:-1]):
        if axis in AG_DIRECT:
            piece = _ag_direct(piece, axis, size)
        else:
            piece = _ag_stage(piece, axis, size)
        piece, kept[i] = lax.optimization_barrier((piece, kept[i]))
    gate_kept, up_kept, down_kept = kept
    last = AG_ORDER[-1]
    _, n_last = BLK_AXES[last]
    assert n_last == 2
    blocks = [piece, lax.ppermute(piece, "blk", _perm(last, 1, size))]
    gate = jnp.concatenate(
        [jnp.dot(b, gate_kept, preferred_element_type=jnp.float32) for b in blocks], axis=0)
    up_val = jnp.concatenate(
        [jnp.dot(b, up_kept, preferred_element_type=jnp.float32) for b in blocks], axis=0)
    hidden = (jax.nn.silu(gate) * up_val).astype(jnp.bfloat16)

    outs = []
    lo = 0
    for groups, rs_order, direct in PARTS:
        hi = lo + groups * 128
        h = hidden if rs_order == base else _reorder_rows(hidden, base, rs_order, t)
        x = jnp.dot(h, down_kept[:, lo:hi], preferred_element_type=jnp.float32)
        for axis in rs_order:
            if axis in direct:
                x = _rs_direct(x, axis, size)
            else:
                x = _rs_stage(x, axis, size)
        outs.append(x)
        lo = hi
    summed = jnp.concatenate(outs, axis=1) if len(outs) > 1 else outs[0]
    return summed.astype(jnp.bfloat16)


def solution(mesh):
    assert mesh.shape["blk"] == 128
    return jax.shard_map(
        local,
        mesh=mesh,
        in_specs=(
            P(("blk", "rows"), None),
            P(),
            P(None, "blk"),
            P(None, "blk"),
            P("blk", None),
            P(None, "blk"),
            P(None, "blk"),
            P("blk", None),
        ),
        out_specs=P(("blk", "rows"), None),
        check_vma=False,
    )
```

```python
import jax
import jax.numpy as jnp
from jax import lax
from jax.sharding import PartitionSpec as P

BLK_AXES = {"z": (16, 8), "xh": (8, 2), "y": (2, 4), "c": (1, 2)}
AG_ORDER = ("xh", "y", "z", "c")
AG_DIRECT = ("y",)
PARTS = (
    (32, ("c", "z", "y", "xh"), ("y",)),
    (32, ("c", "y", "z", "xh"), ("z",)),
)


def mask_blocks(weight, flags):
    height, width = weight.shape
    down_n = flags.shape[0]
    across_n = flags.shape[1]
    cols = jnp.repeat(flags.astype(weight.dtype), width // across_n, axis=1)
    shaped = weight.reshape(down_n, height // down_n, width)
    return (shaped * cols[:, None, :]).reshape(height, width)


def _perm(axis, k, size):
    stride, n = BLK_AXES[axis]
    cstride = BLK_AXES["c"][0]
    pairs = []
    for i in range(size):
        kk = k if (i // cstride) % 2 == 0 else -k
        coord = (i // stride) % n
        pairs.append((i, i + ((coord + kk) % n - coord) * stride))
    return pairs


def _ag_stage(block, axis, size):
    _, n = BLK_AXES[axis]
    m_plus = n // 2
    m_minus = n - 1 - m_plus
    got = [None] * n
    got[0] = block
    cur = block
    for s in range(m_plus):
        cur = lax.ppermute(cur, "blk", _perm(axis, 1, size))
        got[n - s - 1] = cur
    cur = block
    for s in range(m_minus):
        cur = lax.ppermute(cur, "blk", _perm(axis, -1, size))
        got[s + 1] = cur
    return jnp.concatenate(got, axis=0)


def _ag_direct(block, axis, size):
    _, n = BLK_AXES[axis]
    got = [block] + [lax.ppermute(block, "blk", _perm(axis, -o, size)) for o in range(1, n)]
    return jnp.concatenate(got, axis=0)


def _rs_direct(x, axis, size):
    _, n = BLK_AXES[axis]
    r = x.shape[0] // n
    total = lax.slice_in_dim(x, 0, r, axis=0)
    for o in range(1, n):
        part = lax.slice_in_dim(x, o * r, (o + 1) * r, axis=0)
        total = total + lax.ppermute(part, "blk", _perm(axis, o, size))
    return total


def _rs_stage(x, axis, size):
    _, n = BLK_AXES[axis]
    r = x.shape[0] // n
    m_plus = n // 2
    m_minus = n - 1 - m_plus

    def take(j):
        return lax.slice_in_dim(x, (j % n) * r, (j % n + 1) * r, axis=0)

    total = take(0)
    buf = take(m_plus)
    for s in range(m_plus):
        recv = lax.ppermute(buf, "blk", _perm(axis, 1, size))
        if s < m_plus - 1:
            buf = recv + take(m_plus - s - 1)
        else:
            total = total + recv
    if m_minus:
        buf = take(n - m_minus)
        for s in range(m_minus):
            recv = lax.ppermute(buf, "blk", _perm(axis, -1, size))
            if s < m_minus - 1:
                buf = recv + take(n - m_minus + s + 1)
            else:
                total = total + recv
    return total


def _reorder_rows(x, src, dst, t):
    sizes = tuple(BLK_AXES[a][1] for a in src) + (t,)
    y = x.reshape(sizes + x.shape[1:])
    perm = [src.index(a) for a in dst] + [len(src)] + [len(src) + 1 + i for i in range(x.ndim - 1)]
    return jnp.transpose(y, perm).reshape(x.shape)


def local(tokens, norm_gain, gate_weight, up_weight, down_weight, gate_mask, up_mask, down_mask):
    size = 1
    for a in BLK_AXES:
        size *= BLK_AXES[a][1]
    t = tokens.shape[0]
    wide_tok = tokens.astype(jnp.float32)
    scale_inv = lax.rsqrt(jnp.mean(wide_tok * wide_tok, axis=-1, keepdims=True) + 1e-05)
    normed = (wide_tok * scale_inv * norm_gain).astype(jnp.bfloat16)
    gate_kept = mask_blocks(gate_weight, gate_mask)
    up_kept = mask_blocks(up_weight, up_mask)
    down_kept = mask_blocks(down_weight, down_mask)

    base = tuple(reversed(AG_ORDER))
    piece = normed
    kept = [gate_kept, up_kept, down_kept]
    for i, axis in enumerate(AG_ORDER[:-1]):
        if axis in AG_DIRECT:
            piece = _ag_direct(piece, axis, size)
        else:
            piece = _ag_stage(piece, axis, size)
        piece, kept[i] = lax.optimization_barrier((piece, kept[i]))
    gate_kept, up_kept, down_kept = kept
    last = AG_ORDER[-1]
    _, n_last = BLK_AXES[last]
    assert n_last == 2
    blocks = [piece, lax.ppermute(piece, "blk", _perm(last, 1, size))]
    gate = jnp.concatenate(
        [jnp.dot(b, gate_kept, preferred_element_type=jnp.float32) for b in blocks], axis=0)
    up_val = jnp.concatenate(
        [jnp.dot(b, up_kept, preferred_element_type=jnp.float32) for b in blocks], axis=0)
    hidden = (jax.nn.silu(gate) * up_val).astype(jnp.bfloat16)

    outs = []
    lo = 0
    for groups, rs_order, direct in PARTS:
        hi = lo + groups * 128
        h = hidden if rs_order == base else _reorder_rows(hidden, base, rs_order, t)
        x = jnp.dot(h, down_kept[:, lo:hi], preferred_element_type=jnp.float32)
        for axis in rs_order:
            if axis in direct:
                x = _rs_direct(x, axis, size)
            else:
                x = _rs_stage(x, axis, size)
        outs.append(x)
        lo = hi
    summed = jnp.concatenate(outs, axis=1) if len(outs) > 1 else outs[0]
    return summed.astype(jnp.bfloat16)


def solution(mesh):
    assert mesh.shape["blk"] == 128
    return jax.shard_map(
        local,
        mesh=mesh,
        in_specs=(
            P(("blk", "rows"), None),
            P(),
            P(None, "blk"),
            P(None, "blk"),
            P("blk", None),
            P(None, "blk"),
            P(None, "blk"),
            P("blk", None),
        ),
        out_specs=P(("blk", "rows"), None),
        check_vma=False,
    )
```

```python
import jax
import jax.numpy as jnp
from jax import lax
from jax.sharding import PartitionSpec as P

BLK_AXES = {"z": (16, 8), "xh": (8, 2), "y": (2, 4), "c": (1, 2)}
AG_ORDER = ("xh", "y", "z", "c")
AG_DIRECT = ("y",)
PARTS = (
    (32, ("c", "z", "y", "xh"), ("y",)),
    (32, ("c", "y", "z", "xh"), ()),
)


def mask_blocks(weight, flags):
    height, width = weight.shape
    down_n = flags.shape[0]
    across_n = flags.shape[1]
    cols = jnp.repeat(flags.astype(weight.dtype), width // across_n, axis=1)
    shaped = weight.reshape(down_n, height // down_n, width)
    return (shaped * cols[:, None, :]).reshape(height, width)


def _perm(axis, k, size):
    stride, n = BLK_AXES[axis]
    cstride = BLK_AXES["c"][0]
    pairs = []
    for i in range(size):
        kk = k if (i // cstride) % 2 == 0 else -k
        coord = (i // stride) % n
        pairs.append((i, i + ((coord + kk) % n - coord) * stride))
    return pairs


def _ag_stage(block, axis, size):
    _, n = BLK_AXES[axis]
    m_plus = n // 2
    m_minus = n - 1 - m_plus
    got = [None] * n
    got[0] = block
    cur = block
    for s in range(m_plus):
        cur = lax.ppermute(cur, "blk", _perm(axis, 1, size))
        got[n - s - 1] = cur
    cur = block
    for s in range(m_minus):
        cur = lax.ppermute(cur, "blk", _perm(axis, -1, size))
        got[s + 1] = cur
    return jnp.concatenate(got, axis=0)


def _ag_direct(block, axis, size):
    _, n = BLK_AXES[axis]
    got = [block] + [lax.ppermute(block, "blk", _perm(axis, -o, size)) for o in range(1, n)]
    return jnp.concatenate(got, axis=0)


def _rs_direct(x, axis, size):
    _, n = BLK_AXES[axis]
    r = x.shape[0] // n
    total = lax.slice_in_dim(x, 0, r, axis=0)
    for o in range(1, n):
        part = lax.slice_in_dim(x, o * r, (o + 1) * r, axis=0)
        total = total + lax.ppermute(part, "blk", _perm(axis, o, size))
    return total


def _rs_stage(x, axis, size):
    _, n = BLK_AXES[axis]
    r = x.shape[0] // n
    m_plus = n // 2
    m_minus = n - 1 - m_plus

    def take(j):
        return lax.slice_in_dim(x, (j % n) * r, (j % n + 1) * r, axis=0)

    total = take(0)
    buf = take(m_plus)
    for s in range(m_plus):
        recv = lax.ppermute(buf, "blk", _perm(axis, 1, size))
        if s < m_plus - 1:
            buf = recv + take(m_plus - s - 1)
        else:
            total = total + recv
    if m_minus:
        buf = take(n - m_minus)
        for s in range(m_minus):
            recv = lax.ppermute(buf, "blk", _perm(axis, -1, size))
            if s < m_minus - 1:
                buf = recv + take(n - m_minus + s + 1)
            else:
                total = total + recv
    return total


def _reorder_rows(x, src, dst, t):
    sizes = tuple(BLK_AXES[a][1] for a in src) + (t,)
    y = x.reshape(sizes + x.shape[1:])
    perm = [src.index(a) for a in dst] + [len(src)] + [len(src) + 1 + i for i in range(x.ndim - 1)]
    return jnp.transpose(y, perm).reshape(x.shape)


def local(tokens, norm_gain, gate_weight, up_weight, down_weight, gate_mask, up_mask, down_mask):
    size = 1
    for a in BLK_AXES:
        size *= BLK_AXES[a][1]
    t = tokens.shape[0]
    wide_tok = tokens.astype(jnp.float32)
    scale_inv = lax.rsqrt(jnp.mean(wide_tok * wide_tok, axis=-1, keepdims=True) + 1e-05)
    normed = (wide_tok * scale_inv * norm_gain).astype(jnp.bfloat16)
    gate_kept = mask_blocks(gate_weight, gate_mask)
    up_kept = mask_blocks(up_weight, up_mask)
    down_kept = mask_blocks(down_weight, down_mask)

    base = tuple(reversed(AG_ORDER))
    piece = normed
    kept = [gate_kept, up_kept, down_kept]
    for i, axis in enumerate(AG_ORDER[:-1]):
        if axis in AG_DIRECT:
            piece = _ag_direct(piece, axis, size)
        else:
            piece = _ag_stage(piece, axis, size)
        piece, kept[i] = lax.optimization_barrier((piece, kept[i]))
    gate_kept, up_kept, down_kept = kept
    last = AG_ORDER[-1]
    _, n_last = BLK_AXES[last]
    assert n_last == 2
    blocks = [piece, lax.ppermute(piece, "blk", _perm(last, 1, size))]
    gate = jnp.concatenate(
        [jnp.dot(b, gate_kept, preferred_element_type=jnp.float32) for b in blocks], axis=0)
    up_val = jnp.concatenate(
        [jnp.dot(b, up_kept, preferred_element_type=jnp.float32) for b in blocks], axis=0)
    hidden = (jax.nn.silu(gate) * up_val).astype(jnp.bfloat16)

    outs = []
    lo = 0
    for groups, rs_order, direct in PARTS:
        hi = lo + groups * 128
        h = hidden if rs_order == base else _reorder_rows(hidden, base, rs_order, t)
        first = rs_order[0]
        assert first == base[0] and BLK_AXES[first][1] == 2
        half = h.shape[0] // 2
        sent = jnp.dot(h[half:], down_kept[:, lo:hi], preferred_element_type=jnp.float32)
        recv = lax.ppermute(sent, "blk", _perm(first, 1, size))
        x = jnp.dot(h[:half], down_kept[:, lo:hi], preferred_element_type=jnp.float32) + recv
        for axis in rs_order[1:]:
            if axis in direct:
                x = _rs_direct(x, axis, size)
            else:
                x = _rs_stage(x, axis, size)
        outs.append(x)
        lo = hi
    summed = jnp.concatenate(outs, axis=1) if len(outs) > 1 else outs[0]
    return summed.astype(jnp.bfloat16)


def solution(mesh):
    assert mesh.shape["blk"] == 128
    return jax.shard_map(
        local,
        mesh=mesh,
        in_specs=(
            P(("blk", "rows"), None),
            P(),
            P(None, "blk"),
            P(None, "blk"),
            P("blk", None),
            P(None, "blk"),
            P(None, "blk"),
            P("blk", None),
        ),
        out_specs=P(("blk", "rows"), None),
        check_vma=False,
    )
```

```python
import jax
import jax.numpy as jnp
from jax import lax
from jax.sharding import PartitionSpec as P

BLK_AXES = {"z": (16, 8), "xh": (8, 2), "y": (2, 4), "c": (1, 2)}
AG_ORDER = ("xh", "y", "z", "c")
AG_DIRECT = ("y",)
PARTS = (
    (34, ("c", "z", "y", "xh"), ("y",)),
    (30, ("c", "y", "z", "xh"), ()),
)


def mask_blocks(weight, flags):
    height, width = weight.shape
    down_n = flags.shape[0]
    across_n = flags.shape[1]
    cols = jnp.repeat(flags.astype(weight.dtype), width // across_n, axis=1)
    shaped = weight.reshape(down_n, height // down_n, width)
    return (shaped * cols[:, None, :]).reshape(height, width)


def _perm(axis, k, size):
    stride, n = BLK_AXES[axis]
    cstride = BLK_AXES["c"][0]
    pairs = []
    for i in range(size):
        kk = k if (i // cstride) % 2 == 0 else -k
        coord = (i // stride) % n
        pairs.append((i, i + ((coord + kk) % n - coord) * stride))
    return pairs


def _ag_stage(block, axis, size):
    _, n = BLK_AXES[axis]
    m_plus = n // 2
    m_minus = n - 1 - m_plus
    got = [None] * n
    got[0] = block
    cur = block
    for s in range(m_plus):
        cur = lax.ppermute(cur, "blk", _perm(axis, 1, size))
        got[n - s - 1] = cur
    cur = block
    for s in range(m_minus):
        cur = lax.ppermute(cur, "blk", _perm(axis, -1, size))
        got[s + 1] = cur
    return jnp.concatenate(got, axis=0)


def _ag_direct(block, axis, size):
    _, n = BLK_AXES[axis]
    got = [block] + [lax.ppermute(block, "blk", _perm(axis, -o, size)) for o in range(1, n)]
    return jnp.concatenate(got, axis=0)


def _rs_direct(x, axis, size):
    _, n = BLK_AXES[axis]
    r = x.shape[0] // n
    total = lax.slice_in_dim(x, 0, r, axis=0)
    for o in range(1, n):
        part = lax.slice_in_dim(x, o * r, (o + 1) * r, axis=0)
        total = total + lax.ppermute(part, "blk", _perm(axis, o, size))
    return total


def _rs_stage(x, axis, size):
    _, n = BLK_AXES[axis]
    r = x.shape[0] // n
    m_plus = n // 2
    m_minus = n - 1 - m_plus

    def take(j):
        return lax.slice_in_dim(x, (j % n) * r, (j % n + 1) * r, axis=0)

    total = take(0)
    buf = take(m_plus)
    for s in range(m_plus):
        recv = lax.ppermute(buf, "blk", _perm(axis, 1, size))
        if s < m_plus - 1:
            buf = recv + take(m_plus - s - 1)
        else:
            total = total + recv
    if m_minus:
        buf = take(n - m_minus)
        for s in range(m_minus):
            recv = lax.ppermute(buf, "blk", _perm(axis, -1, size))
            if s < m_minus - 1:
                buf = recv + take(n - m_minus + s + 1)
            else:
                total = total + recv
    return total


def _reorder_rows(x, src, dst, t):
    sizes = tuple(BLK_AXES[a][1] for a in src) + (t,)
    y = x.reshape(sizes + x.shape[1:])
    perm = [src.index(a) for a in dst] + [len(src)] + [len(src) + 1 + i for i in range(x.ndim - 1)]
    return jnp.transpose(y, perm).reshape(x.shape)


def local(tokens, norm_gain, gate_weight, up_weight, down_weight, gate_mask, up_mask, down_mask):
    size = 1
    for a in BLK_AXES:
        size *= BLK_AXES[a][1]
    t = tokens.shape[0]
    wide_tok = tokens.astype(jnp.float32)
    scale_inv = lax.rsqrt(jnp.mean(wide_tok * wide_tok, axis=-1, keepdims=True) + 1e-05)
    normed = (wide_tok * scale_inv * norm_gain).astype(jnp.bfloat16)
    gate_kept = mask_blocks(gate_weight, gate_mask)
    up_kept = mask_blocks(up_weight, up_mask)
    down_kept = mask_blocks(down_weight, down_mask)

    base = tuple(reversed(AG_ORDER))
    piece = normed
    kept = [gate_kept, up_kept, down_kept]
    for i, axis in enumerate(AG_ORDER[:-1]):
        if axis in AG_DIRECT:
            piece = _ag_direct(piece, axis, size)
        else:
            piece = _ag_stage(piece, axis, size)
        piece, kept[i] = lax.optimization_barrier((piece, kept[i]))
    gate_kept, up_kept, down_kept = kept
    last = AG_ORDER[-1]
    _, n_last = BLK_AXES[last]
    assert n_last == 2
    blocks = [piece, lax.ppermute(piece, "blk", _perm(last, 1, size))]
    gate = jnp.concatenate(
        [jnp.dot(b, gate_kept, preferred_element_type=jnp.float32) for b in blocks], axis=0)
    up_val = jnp.concatenate(
        [jnp.dot(b, up_kept, preferred_element_type=jnp.float32) for b in blocks], axis=0)
    hidden = (jax.nn.silu(gate) * up_val).astype(jnp.bfloat16)

    outs = []
    lo = 0
    for groups, rs_order, direct in PARTS:
        hi = lo + groups * 128
        h = hidden if rs_order == base else _reorder_rows(hidden, base, rs_order, t)
        x = jnp.dot(h, down_kept[:, lo:hi], preferred_element_type=jnp.float32)
        for axis in rs_order:
            if axis in direct:
                x = _rs_direct(x, axis, size)
            else:
                x = _rs_stage(x, axis, size)
        outs.append(x)
        lo = hi
    summed = jnp.concatenate(outs, axis=1) if len(outs) > 1 else outs[0]
    return summed.astype(jnp.bfloat16)


def solution(mesh):
    assert mesh.shape["blk"] == 128
    return jax.shard_map(
        local,
        mesh=mesh,
        in_specs=(
            P(("blk", "rows"), None),
            P(),
            P(None, "blk"),
            P(None, "blk"),
            P("blk", None),
            P(None, "blk"),
            P(None, "blk"),
            P("blk", None),
        ),
        out_specs=P(("blk", "rows"), None),
        check_vma=False,
    )
```

```python
import jax
import jax.numpy as jnp
from jax import lax
from jax.sharding import PartitionSpec as P

BLK_AXES = {"z": (16, 8), "xh": (8, 2), "y": (2, 4), "c": (1, 2)}
AG_ORDER = ("xh", "y", "z", "c")
AG_DIRECT = ("y",)
PARTS = (
    (32, ("c", "z", "y", "xh"), ("y",)),
    (32, ("c", "y", "z", "xh"), ("y",)),
)


def mask_blocks(weight, flags):
    height, width = weight.shape
    down_n = flags.shape[0]
    across_n = flags.shape[1]
    cols = jnp.repeat(flags.astype(weight.dtype), width // across_n, axis=1)
    shaped = weight.reshape(down_n, height // down_n, width)
    return (shaped * cols[:, None, :]).reshape(height, width)


def _perm(axis, k, size):
    stride, n = BLK_AXES[axis]
    cstride = BLK_AXES["c"][0]
    pairs = []
    for i in range(size):
        kk = k if (i // cstride) % 2 == 0 else -k
        coord = (i // stride) % n
        pairs.append((i, i + ((coord + kk) % n - coord) * stride))
    return pairs


def _ag_stage(block, axis, size):
    _, n = BLK_AXES[axis]
    m_plus = n // 2
    m_minus = n - 1 - m_plus
    got = [None] * n
    got[0] = block
    cur = block
    for s in range(m_plus):
        cur = lax.ppermute(cur, "blk", _perm(axis, 1, size))
        got[n - s - 1] = cur
    cur = block
    for s in range(m_minus):
        cur = lax.ppermute(cur, "blk", _perm(axis, -1, size))
        got[s + 1] = cur
    return jnp.concatenate(got, axis=0)


def _ag_direct(block, axis, size):
    _, n = BLK_AXES[axis]
    got = [block] + [lax.ppermute(block, "blk", _perm(axis, -o, size)) for o in range(1, n)]
    return jnp.concatenate(got, axis=0)


def _rs_direct(x, axis, size):
    _, n = BLK_AXES[axis]
    r = x.shape[0] // n
    total = lax.slice_in_dim(x, 0, r, axis=0)
    for o in range(1, n):
        part = lax.slice_in_dim(x, o * r, (o + 1) * r, axis=0)
        total = total + lax.ppermute(part, "blk", _perm(axis, o, size))
    return total


def _rs_stage(x, axis, size):
    _, n = BLK_AXES[axis]
    r = x.shape[0] // n
    m_plus = n // 2
    m_minus = n - 1 - m_plus

    def take(j):
        return lax.slice_in_dim(x, (j % n) * r, (j % n + 1) * r, axis=0)

    total = take(0)
    buf = take(m_plus)
    for s in range(m_plus):
        recv = lax.ppermute(buf, "blk", _perm(axis, 1, size))
        if s < m_plus - 1:
            buf = recv + take(m_plus - s - 1)
        else:
            total = total + recv
    if m_minus:
        buf = take(n - m_minus)
        for s in range(m_minus):
            recv = lax.ppermute(buf, "blk", _perm(axis, -1, size))
            if s < m_minus - 1:
                buf = recv + take(n - m_minus + s + 1)
            else:
                total = total + recv
    return total


def _reorder_rows(x, src, dst, t):
    sizes = tuple(BLK_AXES[a][1] for a in src) + (t,)
    y = x.reshape(sizes + x.shape[1:])
    perm = [src.index(a) for a in dst] + [len(src)] + [len(src) + 1 + i for i in range(x.ndim - 1)]
    return jnp.transpose(y, perm).reshape(x.shape)


def local(tokens, norm_gain, gate_weight, up_weight, down_weight, gate_mask, up_mask, down_mask):
    size = 1
    for a in BLK_AXES:
        size *= BLK_AXES[a][1]
    t = tokens.shape[0]
    wide_tok = tokens.astype(jnp.float32)
    scale_inv = lax.rsqrt(jnp.mean(wide_tok * wide_tok, axis=-1, keepdims=True) + 1e-05)
    normed = (wide_tok * scale_inv * norm_gain).astype(jnp.bfloat16)
    gate_kept = mask_blocks(gate_weight, gate_mask)
    up_kept = mask_blocks(up_weight, up_mask)
    down_kept = mask_blocks(down_weight, down_mask)

    base = tuple(reversed(AG_ORDER))
    piece = normed
    kept = [gate_kept, up_kept, down_kept]
    for i, axis in enumerate(AG_ORDER[:-1]):
        if axis in AG_DIRECT:
            piece = _ag_direct(piece, axis, size)
        else:
            piece = _ag_stage(piece, axis, size)
        piece, kept[i] = lax.optimization_barrier((piece, kept[i]))
    gate_kept, up_kept, down_kept = kept
    last = AG_ORDER[-1]
    _, n_last = BLK_AXES[last]
    assert n_last == 2
    blocks = [piece, lax.ppermute(piece, "blk", _perm(last, 1, size))]
    gate = jnp.concatenate(
        [jnp.dot(b, gate_kept, preferred_element_type=jnp.float32) for b in blocks], axis=0)
    up_val = jnp.concatenate(
        [jnp.dot(b, up_kept, preferred_element_type=jnp.float32) for b in blocks], axis=0)
    hidden = (jax.nn.silu(gate) * up_val).astype(jnp.bfloat16)

    outs = []
    lo = 0
    for groups, rs_order, direct in PARTS:
        hi = lo + groups * 128
        h = hidden if rs_order == base else _reorder_rows(hidden, base, rs_order, t)
        x = jnp.dot(h, down_kept[:, lo:hi], preferred_element_type=jnp.float32)
        for axis in rs_order:
            if axis in direct:
                x = _rs_direct(x, axis, size)
            else:
                x = _rs_stage(x, axis, size)
        outs.append(x)
        lo = hi
    summed = jnp.concatenate(outs, axis=1) if len(outs) > 1 else outs[0]
    return summed.astype(jnp.bfloat16)


def solution(mesh):
    assert mesh.shape["blk"] == 128
    return jax.shard_map(
        local,
        mesh=mesh,
        in_specs=(
            P(("blk", "rows"), None),
            P(),
            P(None, "blk"),
            P(None, "blk"),
            P("blk", None),
            P(None, "blk"),
            P(None, "blk"),
            P("blk", None),
        ),
        out_specs=P(("blk", "rows"), None),
        check_vma=False,
    )
```

```python
import jax
import jax.numpy as jnp
from jax import lax
from jax.sharding import PartitionSpec as P

BLK_AXES = {"z": (16, 8), "xh": (8, 2), "y": (2, 4), "c": (1, 2)}
AG_ORDER = ("xh", "y", "z", "c")
AG_DIRECT = ("y",)
PARTS = (
    (32, ("c", "z", "y", "xh"), ("y",)),
    (32, ("c", "y", "z", "xh"), ()),
)


def mask_blocks(weight, flags):
    height, width = weight.shape
    down_n = flags.shape[0]
    across_n = flags.shape[1]
    cols = jnp.repeat(flags.astype(weight.dtype), width // across_n, axis=1)
    shaped = weight.reshape(down_n, height // down_n, width)
    return (shaped * cols[:, None, :]).reshape(height, width)


def _perm(axis, k, size):
    stride, n = BLK_AXES[axis]
    cstride = BLK_AXES["c"][0]
    pairs = []
    for i in range(size):
        kk = k if (i // cstride) % 2 == 0 else -k
        coord = (i // stride) % n
        pairs.append((i, i + ((coord + kk) % n - coord) * stride))
    return pairs


def _ag_stage(block, axis, size):
    _, n = BLK_AXES[axis]
    m_plus = n // 2
    m_minus = n - 1 - m_plus
    got = [None] * n
    got[0] = block
    cur = block
    for s in range(m_plus):
        cur = lax.ppermute(cur, "blk", _perm(axis, 1, size))
        got[n - s - 1] = cur
    cur = block
    for s in range(m_minus):
        cur = lax.ppermute(cur, "blk", _perm(axis, -1, size))
        got[s + 1] = cur
    return jnp.concatenate(got, axis=0)


def _ag_direct(block, axis, size):
    _, n = BLK_AXES[axis]
    got = [block] + [lax.ppermute(block, "blk", _perm(axis, -o, size)) for o in range(1, n)]
    return jnp.concatenate(got, axis=0)


def _rs_direct(x, axis, size):
    _, n = BLK_AXES[axis]
    r = x.shape[0] // n
    total = lax.slice_in_dim(x, 0, r, axis=0)
    for o in range(1, n):
        part = lax.slice_in_dim(x, o * r, (o + 1) * r, axis=0)
        total = total + lax.ppermute(part, "blk", _perm(axis, o, size))
    return total


def _rs_stage(x, axis, size):
    _, n = BLK_AXES[axis]
    r = x.shape[0] // n
    m_plus = n // 2
    m_minus = n - 1 - m_plus

    def take(j):
        return lax.slice_in_dim(x, (j % n) * r, (j % n + 1) * r, axis=0)

    total = take(0)
    buf = take(m_plus)
    for s in range(m_plus):
        recv = lax.ppermute(buf, "blk", _perm(axis, 1, size))
        if s < m_plus - 1:
            buf = recv + take(m_plus - s - 1)
        else:
            total = total + recv
    if m_minus:
        buf = take(n - m_minus)
        for s in range(m_minus):
            recv = lax.ppermute(buf, "blk", _perm(axis, -1, size))
            if s < m_minus - 1:
                buf = recv + take(n - m_minus + s + 1)
            else:
                total = total + recv
    return total


def _reorder_rows(x, src, dst, t):
    sizes = tuple(BLK_AXES[a][1] for a in src) + (t,)
    y = x.reshape(sizes + x.shape[1:])
    perm = [src.index(a) for a in dst] + [len(src)] + [len(src) + 1 + i for i in range(x.ndim - 1)]
    return jnp.transpose(y, perm).reshape(x.shape)


def local(tokens, norm_gain, gate_weight, up_weight, down_weight, gate_mask, up_mask, down_mask):
    size = 1
    for a in BLK_AXES:
        size *= BLK_AXES[a][1]
    t = tokens.shape[0]
    wide_tok = tokens.astype(jnp.float32)
    scale_inv = lax.rsqrt(jnp.mean(wide_tok * wide_tok, axis=-1, keepdims=True) + 1e-05)
    normed = (wide_tok * scale_inv * norm_gain).astype(jnp.bfloat16)
    gate_kept = mask_blocks(gate_weight, gate_mask)
    up_kept = mask_blocks(up_weight, up_mask)
    down_kept = mask_blocks(down_weight, down_mask)

    base = tuple(reversed(AG_ORDER))
    piece = normed
    kept = [down_kept, up_kept, gate_kept]
    for i, axis in enumerate(AG_ORDER[:-1]):
        if axis in AG_DIRECT:
            piece = _ag_direct(piece, axis, size)
        else:
            piece = _ag_stage(piece, axis, size)
        piece, kept[i] = lax.optimization_barrier((piece, kept[i]))
    down_kept, up_kept, gate_kept = kept
    last = AG_ORDER[-1]
    _, n_last = BLK_AXES[last]
    assert n_last == 2
    blocks = [piece, lax.ppermute(piece, "blk", _perm(last, 1, size))]
    gate = jnp.concatenate(
        [jnp.dot(b, gate_kept, preferred_element_type=jnp.float32) for b in blocks], axis=0)
    up_val = jnp.concatenate(
        [jnp.dot(b, up_kept, preferred_element_type=jnp.float32) for b in blocks], axis=0)
    hidden = (jax.nn.silu(gate) * up_val).astype(jnp.bfloat16)

    outs = []
    lo = 0
    for groups, rs_order, direct in PARTS:
        hi = lo + groups * 128
        h = hidden if rs_order == base else _reorder_rows(hidden, base, rs_order, t)
        x = jnp.dot(h, down_kept[:, lo:hi], preferred_element_type=jnp.float32)
        for axis in rs_order:
            if axis in direct:
                x = _rs_direct(x, axis, size)
            else:
                x = _rs_stage(x, axis, size)
        outs.append(x)
        lo = hi
    summed = jnp.concatenate(outs, axis=1) if len(outs) > 1 else outs[0]
    return summed.astype(jnp.bfloat16)


def solution(mesh):
    assert mesh.shape["blk"] == 128
    return jax.shard_map(
        local,
        mesh=mesh,
        in_specs=(
            P(("blk", "rows"), None),
            P(),
            P(None, "blk"),
            P(None, "blk"),
            P("blk", None),
            P(None, "blk"),
            P(None, "blk"),
            P("blk", None),
        ),
        out_specs=P(("blk", "rows"), None),
        check_vma=False,
    )
```

```python
import jax
import jax.numpy as jnp
from jax import lax
from jax.sharding import PartitionSpec as P

BLK_AXES = {"z": (16, 8), "xh": (8, 2), "y": (2, 4), "c": (1, 2)}
AG_ORDER = ("xh", "y", "z", "c")
AG_DIRECT = ("y",)
PARTS = (
    (32, ("c", "z", "y", "xh"), ("y",)),
    (32, ("c", "y", "z", "xh"), ()),
)


def mask_blocks(weight, flags):
    height, width = weight.shape
    down_n = flags.shape[0]
    across_n = flags.shape[1]
    cols = jnp.repeat(flags.astype(weight.dtype), width // across_n, axis=1)
    shaped = weight.reshape(down_n, height // down_n, width)
    return (shaped * cols[:, None, :]).reshape(height, width)


def _perm(axis, k, size):
    stride, n = BLK_AXES[axis]
    cstride = BLK_AXES["c"][0]
    pairs = []
    for i in range(size):
        kk = k if (i // cstride) % 2 == 0 else -k
        coord = (i // stride) % n
        pairs.append((i, i + ((coord + kk) % n - coord) * stride))
    return pairs


def _ag_stage(block, axis, size):
    _, n = BLK_AXES[axis]
    m_plus = n // 2
    m_minus = n - 1 - m_plus
    got = [None] * n
    got[0] = block
    cur = block
    for s in range(m_plus):
        cur = lax.ppermute(cur, "blk", _perm(axis, 1, size))
        got[n - s - 1] = cur
    cur = block
    for s in range(m_minus):
        cur = lax.ppermute(cur, "blk", _perm(axis, -1, size))
        got[s + 1] = cur
    return jnp.concatenate(got, axis=0)


def _ag_direct(block, axis, size):
    _, n = BLK_AXES[axis]
    got = [block] + [lax.ppermute(block, "blk", _perm(axis, -o, size)) for o in range(1, n)]
    return jnp.concatenate(got, axis=0)


def _rs_direct(x, axis, size):
    _, n = BLK_AXES[axis]
    r = x.shape[0] // n
    total = lax.slice_in_dim(x, 0, r, axis=0)
    for o in range(1, n):
        part = lax.slice_in_dim(x, o * r, (o + 1) * r, axis=0)
        total = total + lax.ppermute(part, "blk", _perm(axis, o, size))
    return total


def _rs_stage(x, axis, size):
    _, n = BLK_AXES[axis]
    r = x.shape[0] // n
    m_minus = n // 2
    m_plus = n - 1 - m_minus

    def take(j):
        return lax.slice_in_dim(x, (j % n) * r, (j % n + 1) * r, axis=0)

    total = take(0)
    buf = take(m_plus)
    for s in range(m_plus):
        recv = lax.ppermute(buf, "blk", _perm(axis, 1, size))
        if s < m_plus - 1:
            buf = recv + take(m_plus - s - 1)
        else:
            total = total + recv
    if m_minus:
        buf = take(n - m_minus)
        for s in range(m_minus):
            recv = lax.ppermute(buf, "blk", _perm(axis, -1, size))
            if s < m_minus - 1:
                buf = recv + take(n - m_minus + s + 1)
            else:
                total = total + recv
    return total


def _reorder_rows(x, src, dst, t):
    sizes = tuple(BLK_AXES[a][1] for a in src) + (t,)
    y = x.reshape(sizes + x.shape[1:])
    perm = [src.index(a) for a in dst] + [len(src)] + [len(src) + 1 + i for i in range(x.ndim - 1)]
    return jnp.transpose(y, perm).reshape(x.shape)


def local(tokens, norm_gain, gate_weight, up_weight, down_weight, gate_mask, up_mask, down_mask):
    size = 1
    for a in BLK_AXES:
        size *= BLK_AXES[a][1]
    t = tokens.shape[0]
    wide_tok = tokens.astype(jnp.float32)
    scale_inv = lax.rsqrt(jnp.mean(wide_tok * wide_tok, axis=-1, keepdims=True) + 1e-05)
    normed = (wide_tok * scale_inv * norm_gain).astype(jnp.bfloat16)
    gate_kept = mask_blocks(gate_weight, gate_mask)
    up_kept = mask_blocks(up_weight, up_mask)
    down_kept = mask_blocks(down_weight, down_mask)

    base = tuple(reversed(AG_ORDER))
    piece = normed
    kept = [gate_kept, up_kept, down_kept]
    for i, axis in enumerate(AG_ORDER[:-1]):
        if axis in AG_DIRECT:
            piece = _ag_direct(piece, axis, size)
        else:
            piece = _ag_stage(piece, axis, size)
        piece, kept[i] = lax.optimization_barrier((piece, kept[i]))
    gate_kept, up_kept, down_kept = kept
    last = AG_ORDER[-1]
    _, n_last = BLK_AXES[last]
    assert n_last == 2
    blocks = [piece, lax.ppermute(piece, "blk", _perm(last, 1, size))]
    gate = jnp.concatenate(
        [jnp.dot(b, gate_kept, preferred_element_type=jnp.float32) for b in blocks], axis=0)
    up_val = jnp.concatenate(
        [jnp.dot(b, up_kept, preferred_element_type=jnp.float32) for b in blocks], axis=0)
    hidden = (jax.nn.silu(gate) * up_val).astype(jnp.bfloat16)

    outs = []
    lo = 0
    for groups, rs_order, direct in PARTS:
        hi = lo + groups * 128
        h = hidden if rs_order == base else _reorder_rows(hidden, base, rs_order, t)
        x = jnp.dot(h, down_kept[:, lo:hi], preferred_element_type=jnp.float32)
        for axis in rs_order:
            if axis in direct:
                x = _rs_direct(x, axis, size)
            else:
                x = _rs_stage(x, axis, size)
        outs.append(x)
        lo = hi
    summed = jnp.concatenate(outs, axis=1) if len(outs) > 1 else outs[0]
    return summed.astype(jnp.bfloat16)


def solution(mesh):
    assert mesh.shape["blk"] == 128
    return jax.shard_map(
        local,
        mesh=mesh,
        in_specs=(
            P(("blk", "rows"), None),
            P(),
            P(None, "blk"),
            P(None, "blk"),
            P("blk", None),
            P(None, "blk"),
            P(None, "blk"),
            P("blk", None),
        ),
        out_specs=P(("blk", "rows"), None),
        check_vma=False,
    )
```
